128 devices in a mesh: grp: 4 (over y_lo, core), band: 32 (over y_hi, x, z).
Axes of the slice: x: 4, y: 4 (y_hi: 2, y_lo: 2; y = y_hi * 2 + y_lo), z: 4, core: 2. Of those that a mesh axis runs over, the one named last changes fastest.
Arguments:
- prior_samples: bfloat16 [32, 69, 64, 1024], P('grp', None, 'band'), may hold values from -6 to 6
- conv1_weight: bfloat16 [3, 3, 256, 69], replicated, may hold values from -0.25 to 0.25
- conv1_bias: float32 [256], replicated, may hold values from -3 to 3
- conv2_weight: bfloat16 [3, 3, 69, 256], replicated, may hold values from -0.125 to 0.125
- conv2_bias: float32 [69], replicated, may hold values from -3 to 3
- obs_index: int32 [256, 256], P(('grp', 'band')), may hold values from 0 to 17663
- obs_values: float32 [256, 256], P(('grp', 'band')), may hold values from -6 to 6
- obs_prec: float32 [256, 256], P(('grp', 'band')), may hold values from 0.25 to 4
- neighbours: int32 [256, 8], P(('grp', 'band')), may hold values from 0 to 255
- loc_weight: float32 [256, 8], P(('grp', 'band')), may hold values from 0.2 to 1
Outputs:
- analysis: float32 [32, 69, 64, 1024], P(None, None, 'band', 'grp')
The draws below stay inside these ranges and needn't reach their ends.
Inputs may be any that keep to these rules, and one draw needn't show every extreme that they name: `neighbours`: neighbour patch numbers; a number may repeat or name the patch itself. `obs_index`: observed entry as channel * 256 + column within the patch.
All inputs are finite; a program needn't handle non-finite values.
Results may differ from the reference program's by a relative error of at most 0.0021.
Values may be sent and summed in bfloat16 or wider, within the bound.
No kernel may reach another device: no remote copies, remote signals or barrier semaphores. Data moves between devices by JAX's collectives and lax.ppermute only.
A program may use at most 128 MiB of HBM per device.

```python
import math
import jax
import jax.numpy as jnp
from jax import lax

MEMBERS_TOTAL = 32
VARIABLE_TOTAL = 69
HID = 256
TILE_MERIDIANS = 256
NOBS = 256
NBRS = 8
NS_ITERS = 6
PARALLEL_LINES = 64
TILES_ACROSS = 4
LON = 1024
TILE_TOTAL = 256


def set_ends(values, stream_key, least, high):
    place = [jax.random.randint(jax.random.fold_in(stream_key, axis), (), 0, length) for axis, length in enumerate(values.shape)]
    widest = values.shape.index(max(values.shape))
    beside = place[:widest] + [(place[widest] + 1) % values.shape[widest]] + place[widest + 1:]
    return values.at[tuple(place)].set(least).at[tuple(beside)].set(high)


def levels(rng, dims, shards, least, top_value):
    factor_of = 1.0
    for axis_at, blocks in shards:
        heights = jax.random.uniform(jax.random.fold_in(jax.random.fold_in(rng, 6), axis_at), (blocks,), jnp.float32, least / len(shards), top_value / len(shards))
        factor_of = factor_of * jnp.repeat(jnp.exp(heights), dims[axis_at] // blocks).reshape((-1,) + (1,) * (len(dims) - 1 - axis_at))
    return factor_of


def centred(rng, shape, scale, bound, cuts=(), kind=jnp.bfloat16):
    entries = scale * jax.random.normal(rng, shape, jnp.float32)
    if cuts:
        entries = entries * levels(rng, shape, cuts, -0.22, 0.18)
    return jnp.clip(entries, -bound, bound).astype(kind)


def setup_inputs(seed: int = 0) -> dict:
    key_list = jax.random.split(jax.random.key(seed), 11)
    prior_samples = centred(key_list[0], (MEMBERS_TOTAL, VARIABLE_TOTAL, PARALLEL_LINES, LON), 1.0, 6.0, ((0, 4), (2, 32)))
    conv1_weight = centred(key_list[1], (3, 3, HID, VARIABLE_TOTAL), (9 * VARIABLE_TOTAL) ** -0.5, 0.25)
    conv1_bias = centred(key_list[2], (HID,), 0.5, 3.0, (), jnp.float32)
    conv2_weight = centred(key_list[3], (3, 3, VARIABLE_TOTAL, HID), (9 * HID) ** -0.5, 0.125)
    conv2_bias = centred(key_list[4], (VARIABLE_TOTAL,), 0.5, 3.0, (), jnp.float32)
    obs_index = set_ends(jax.random.randint(key_list[5], (TILE_TOTAL, NOBS), 0, VARIABLE_TOTAL * TILE_MERIDIANS), jax.random.fold_in(key_list[5], 1), 0, (VARIABLE_TOTAL * TILE_MERIDIANS) - 1).astype(jnp.int32)
    obs_values = centred(key_list[6], (TILE_TOTAL, NOBS), 1.0, 6.0, ((0, 128),), jnp.float32)
    obs_prec = jnp.clip(jnp.exp(math.log(4.0) - 2.7725887 * jax.random.uniform(key_list[7], (TILE_TOTAL, NOBS), jnp.float32) ** levels(key_list[7], (TILE_TOTAL, NOBS), ((0, 128),), -0.2, 0.2)), 0.25, 4.0)
    neighbours = set_ends(jax.random.randint(key_list[8], (TILE_TOTAL, NBRS), 0, TILE_TOTAL), jax.random.fold_in(key_list[8], 1), 0, TILE_TOTAL - 1).astype(jnp.int32)
    loc_weight = jnp.clip(0.2 + 0.8 * jax.random.uniform(key_list[9], (TILE_TOTAL, NBRS), jnp.float32) ** levels(key_list[9], (TILE_TOTAL, NBRS), ((0, 128),), -0.2, 0.2), 0.2, 1.0)
    return {"prior_samples": prior_samples, "conv1_weight": conv1_weight, "conv1_bias": conv1_bias, "conv2_weight": conv2_weight, "conv2_bias": conv2_bias, "obs_index": obs_index, "obs_values": obs_values, "obs_prec": obs_prec, "neighbours": neighbours, "loc_weight": loc_weight}


def convolve(field, kernel):
    height = field.shape[1]
    padded = jnp.pad(field, ((0, 0), (1, 1), (0, 0)))
    summed = jnp.zeros((kernel.shape[2], height, field.shape[2]), jnp.float32)
    for row_shift in range(3):
        window = padded[:, row_shift:row_shift + height, :]
        for col_shift in range(3):
            shifted = jnp.roll(window, 1 - col_shift, axis=2)
            summed = summed + jnp.einsum('oc,crl->orl', kernel[row_shift, col_shift], shifted)
    return summed

def reference(prior_samples, conv1_weight, conv1_bias, conv2_weight, conv2_bias, obs_index, obs_values, obs_prec, neighbours, loc_weight):
    highest = lax.Precision.HIGHEST
    kernel_one = conv1_weight.astype(jnp.float32)
    kernel_two = conv2_weight.astype(jnp.float32)

    def propagate_realization(member):
        field = member.astype(jnp.float32)
        hidden_fields = jax.nn.silu(convolve(field, kernel_one) + conv1_bias[:, None, None]).astype(jnp.bfloat16)
        hidden_fields = lax.optimization_barrier(hidden_fields).astype(jnp.float32)
        return (field + convolve(hidden_fields, kernel_two) + conv2_bias[:, None, None]).astype(jnp.bfloat16)
    predicted_samples = lax.map(propagate_realization, prior_samples)
    realization_grid = predicted_samples.reshape(MEMBERS_TOTAL, VARIABLE_TOTAL, PARALLEL_LINES, TILES_ACROSS, TILE_MERIDIANS).transpose(3, 2, 0, 1, 4).reshape(TILE_TOTAL, MEMBERS_TOTAL, VARIABLE_TOTAL * TILE_MERIDIANS)
    chosen = jnp.broadcast_to(obs_index[:, None, :], (TILE_TOTAL, MEMBERS_TOTAL, NOBS))
    predicted = jnp.take_along_axis(realization_grid, chosen, axis=2).astype(jnp.float32)
    predicted_mean = lax.optimization_barrier(jnp.mean(predicted, axis=1))
    perturb = predicted - predicted_mean[:, None, :]
    innovation = obs_values - predicted_mean
    gram_local = jnp.einsum('pmo,po,pno->pmn', perturb, obs_prec, perturb, precision=highest)
    pull_vec = jnp.einsum('pmo,po->pm', perturb, obs_prec * innovation, precision=highest)
    identity = jnp.broadcast_to(jnp.eye(MEMBERS_TOTAL, dtype=jnp.float32), (TILE_TOTAL, MEMBERS_TOTAL, MEMBERS_TOTAL))
    matrix = (MEMBERS_TOTAL - 1.0) * identity + gram_local + jnp.einsum('pk,pkmn->pmn', loc_weight, gram_local[neighbours], precision=highest)
    pulled = pull_vec + jnp.einsum('pk,pkm->pm', loc_weight, pull_vec[neighbours], precision=highest)
    norm_scale = jnp.sqrt(lax.optimization_barrier(jnp.sum(matrix * matrix, axis=(1, 2))))
    sqrt_iter = matrix / norm_scale[:, None, None]
    inverse_root = identity
    for sweep in range(NS_ITERS):
        half_step = 1.5 * identity - 0.5 * jnp.einsum('pab,pbc->pac', inverse_root, sqrt_iter, precision=highest)
        sqrt_iter = jnp.einsum('pab,pbc->pac', sqrt_iter, half_step, precision=highest)
        inverse_root = jnp.einsum('pab,pbc->pac', half_step, inverse_root, precision=highest)
    once_applied = jnp.einsum('pab,pb->pa', inverse_root, pulled, precision=highest)
    mean_weight = jnp.einsum('pab,pb->pa', inverse_root, once_applied, precision=highest) / norm_scale[:, None]
    transform = (jnp.sqrt(MEMBERS_TOTAL - 1.0) / jnp.sqrt(norm_scale))[:, None, None] * inverse_root + mean_weight[:, :, None]

    def analyse(pair):
        weight_mat, members = pair
        field = members.astype(jnp.float32)
        centre = lax.optimization_barrier(jnp.mean(field, axis=0))
        spread = field - centre[None, :]
        return centre[None, :] + jnp.einsum('km,kc->mc', weight_mat, spread, precision=highest)
    analysed = lax.map(analyse, (transform, realization_grid))
    return analysed.reshape(TILES_ACROSS, PARALLEL_LINES, MEMBERS_TOTAL, VARIABLE_TOTAL, TILE_MERIDIANS).transpose(2, 3, 1, 0, 4).reshape(MEMBERS_TOTAL, VARIABLE_TOTAL, PARALLEL_LINES, LON)
```

```python
import jax
import jax.numpy as jnp
import numpy as np
from jax import lax
from jax.sharding import Mesh
from jax.sharding import PartitionSpec as P

NS_ITERS = 6

GRP = ("y_lo", "core")
BAND = ("y_hi", "x", "z")
GATHER_ORDER = ("z", "x", "y_hi", "core", "y_lo")


def shift_pairs(count, step):
    return [(i, i + step) for i in range(count) if 0 <= i + step < count]


def padded_2(cells, band_size, width):
    head = lax.slice_in_dim(cells, 0, width, axis=2)
    tail = lax.slice_in_dim(cells, cells.shape[2] - width, cells.shape[2], axis=2)
    return jnp.concatenate(
        [
            lax.ppermute(tail, BAND, shift_pairs(band_size, 1)),
            cells,
            lax.ppermute(head, BAND, shift_pairs(band_size, -1)),
        ],
        axis=2,
    )


def convolve(padded, kernel, height):
    summed = jnp.zeros((kernel.shape[2], height, padded.shape[2]), jnp.float32)
    for row_shift in range(3):
        window = padded[:, row_shift : row_shift + height, :]
        for col_shift in range(3):
            shifted = jnp.roll(window, 1 - col_shift, axis=2)
            summed = summed + jnp.einsum(
                "oc,crl->orl",
                kernel[row_shift, col_shift],
                shifted,
                preferred_element_type=jnp.float32,
            )
    return summed


def make_on_device(band_size):
    def on_device(
        prior_samples,
        conv1_weight,
        conv1_bias,
        conv2_weight,
        conv2_bias,
        obs_index,
        obs_values,
        obs_prec,
        neighbours,
        loc_weight,
    ):
        highest = lax.Precision.HIGHEST
        height = prior_samples.shape[2]
        padded = padded_2(prior_samples, band_size, 1)

        def first_layer(member):
            return jax.nn.silu(
                convolve(member, conv1_weight, height) + conv1_bias[:, None, None]
            ).astype(jnp.bfloat16)

        hidden_fields = lax.map(first_layer, padded)
        northern_halo = lax.ppermute(
            hidden_fields[:, :, height - 1 :, :], BAND, shift_pairs(band_size, 1)
        )
        southern_halo = lax.ppermute(
            hidden_fields[:, :, :1, :], BAND, shift_pairs(band_size, -1)
        )

        def output_layer(inputs):
            member, own_rows, above_row, below_row = inputs
            extended = jnp.concatenate([above_row, own_rows, below_row], axis=1)
            summed = (
                member.astype(jnp.float32)
                + convolve(extended, conv2_weight, height)
                + conv2_bias[:, None, None]
            )
            return summed.astype(jnp.bfloat16)

        predicted_samples = lax.map(
            output_layer, (prior_samples, hidden_fields, northern_halo, southern_halo)
        )
        patch_block_slice = lax.all_to_all(
            predicted_samples, GRP, split_axis=3, concat_axis=0, tiled=True
        )
        ensemble = patch_block_slice.shape[0]
        channels = patch_block_slice.shape[1]
        patch_width = patch_block_slice.shape[3]

        column = obs_index % patch_width
        channel = obs_index // patch_width
        column_hot = (
            column[:, :, None] == jnp.arange(patch_width, dtype=jnp.int32)[None, None, :]
        ).astype(jnp.bfloat16)
        by_column = jnp.einsum(
            "mcil,iol->icmo", patch_block_slice, column_hot,
            preferred_element_type=jnp.float32,
        )
        channel_hot = (
            channel[:, None, :] == jnp.arange(channels, dtype=jnp.int32)[None, :, None]
        ).astype(jnp.float32)
        predicted = jnp.sum(by_column * channel_hot[:, :, None, :], axis=1)

        predicted_mean = jnp.mean(predicted, axis=1)
        perturb = predicted - predicted_mean[:, None, :]
        innovation = obs_values - predicted_mean
        gram_local = jnp.einsum(
            "pmo,po,pno->pmn", perturb, obs_prec, perturb, precision=highest
        )
        pull_vec = jnp.einsum(
            "pmo,po->pm", perturb, obs_prec * innovation, precision=highest
        )
        count = gram_local.shape[0]
        packed = jnp.concatenate(
            [gram_local.reshape(count, ensemble * ensemble), pull_vec], axis=1
        )
        for axis in GATHER_ORDER:
            packed = lax.all_gather(packed, axis, axis=0, tiled=False)
        packed = packed.reshape(-1, ensemble * ensemble + ensemble)
        total_patches = packed.shape[0]
        patch_ids = jnp.arange(total_patches, dtype=jnp.int32)
        matches = (neighbours[:, :, None] == patch_ids[None, None, :]).astype(jnp.float32)
        spread_weights = jnp.sum(loc_weight[:, :, None] * matches, axis=1)
        summed = jnp.einsum("pj,jf->pf", spread_weights, packed, precision=highest)
        gram_sum = summed[:, : ensemble * ensemble].reshape(count, ensemble, ensemble)
        pull_sum = summed[:, ensemble * ensemble :]
        identity = jnp.broadcast_to(
            jnp.eye(ensemble, dtype=jnp.float32), (height, ensemble, ensemble)
        )
        matrix = (ensemble - 1.0) * identity + gram_local + gram_sum
        pulled = pull_vec + pull_sum
        norm_scale = jnp.sqrt(jnp.sum(matrix * matrix, axis=(1, 2)))
        sqrt_iter = matrix / norm_scale[:, None, None]
        inverse_root = identity
        for sweep in range(NS_ITERS):
            half_step = 1.5 * identity - 0.5 * jnp.einsum(
                "pab,pbc->pac", inverse_root, sqrt_iter, precision=highest
            )
            sqrt_iter = jnp.einsum("pab,pbc->pac", sqrt_iter, half_step, precision=highest)
            inverse_root = jnp.einsum("pab,pbc->pac", half_step, inverse_root, precision=highest)
        once_applied = jnp.einsum("pab,pb->pa", inverse_root, pulled, precision=highest)
        mean_weight = (
            jnp.einsum("pab,pb->pa", inverse_root, once_applied, precision=highest)
            / norm_scale[:, None]
        )
        transform = (jnp.sqrt(ensemble - 1.0) / jnp.sqrt(norm_scale))[
            :, None, None
        ] * inverse_root + mean_weight[:, :, None]
        realization_grid = jnp.transpose(patch_block_slice, (2, 0, 1, 3)).reshape(
            height, ensemble, channels * patch_width
        )
        field = realization_grid.astype(jnp.float32)
        centre = jnp.mean(field, axis=1)
        spread = field - centre[:, None, :]
        analysed = centre[:, None, :] + jnp.einsum(
            "pkm,pkc->pmc", transform, spread, precision=highest
        )
        return analysed.reshape(height, ensemble, channels, patch_width).transpose(1, 2, 0, 3)

    return on_device


def solution(mesh):
    grp_size, band_size = mesh.devices.shape
    fine = Mesh(
        mesh.devices.reshape(grp_size // 2, 2, 2, band_size // 32 * 4, 4),
        GRP + BAND,
    )
    placed = (
        P(GRP, None, BAND, None),
        P(),
        P(),
        P(),
        P(),
        P(GRP + BAND, None),
        P(GRP + BAND, None),
        P(GRP + BAND, None),
        P(GRP + BAND, None),
        P(GRP + BAND, None),
    )
    return jax.shard_map(
        make_on_device(band_size),
        mesh=fine,
        in_specs=placed,
        out_specs=P(None, None, BAND, GRP),
        check_vma=False,
    )
```

```python
import jax
import jax.numpy as jnp
import numpy as np
from jax import lax
from jax.sharding import Mesh
from jax.sharding import PartitionSpec as P

NS_ITERS = 6

GRP = ("y_lo", "core")
BAND = ("y_hi", "x", "z")
GATHER_ORDER = ("z", "x", "y_hi", "core", "y_lo")


def shift_pairs(count, step):
    return [(i, i + step) for i in range(count) if 0 <= i + step < count]


def padded_2(cells, band_size, width):
    head = lax.slice_in_dim(cells, 0, width, axis=2)
    tail = lax.slice_in_dim(cells, cells.shape[2] - width, cells.shape[2], axis=2)
    return jnp.concatenate(
        [
            lax.ppermute(tail, BAND, shift_pairs(band_size, 1)),
            cells,
            lax.ppermute(head, BAND, shift_pairs(band_size, -1)),
        ],
        axis=2,
    )


def convolve(padded, kernel):
    wrapped = jnp.concatenate([padded[..., -1:], padded, padded[..., :1]], axis=-1)
    return lax.conv_general_dilated(
        wrapped,
        jnp.transpose(kernel, (2, 3, 0, 1)),
        window_strides=(1, 1),
        padding="VALID",
        dimension_numbers=("NCHW", "OIHW", "NCHW"),
        preferred_element_type=jnp.float32,
    )


def make_on_device(band_size):
    def on_device(
        prior_samples,
        conv1_weight,
        conv1_bias,
        conv2_weight,
        conv2_bias,
        obs_index,
        obs_values,
        obs_prec,
        neighbours,
        loc_weight,
    ):
        highest = lax.Precision.HIGHEST
        height = prior_samples.shape[2]
        padded = padded_2(prior_samples, band_size, 1)

        hidden_fields = jax.nn.silu(
            convolve(padded, conv1_weight) + conv1_bias[None, :, None, None]
        ).astype(jnp.bfloat16)
        northern_halo = lax.ppermute(
            hidden_fields[:, :, height - 1 :, :], BAND, shift_pairs(band_size, 1)
        )
        southern_halo = lax.ppermute(
            hidden_fields[:, :, :1, :], BAND, shift_pairs(band_size, -1)
        )
        extended = jnp.concatenate([northern_halo, hidden_fields, southern_halo], axis=2)
        predicted_samples = (
            prior_samples.astype(jnp.float32)
            + convolve(extended, conv2_weight)
            + conv2_bias[None, :, None, None]
        ).astype(jnp.bfloat16)
        patch_block_slice = lax.all_to_all(
            predicted_samples, GRP, split_axis=3, concat_axis=0, tiled=True
        )
        ensemble = patch_block_slice.shape[0]
        channels = patch_block_slice.shape[1]
        patch_width = patch_block_slice.shape[3]

        column = obs_index % patch_width
        channel = obs_index // patch_width
        column_hot = (
            column[:, :, None] == jnp.arange(patch_width, dtype=jnp.int32)[None, None, :]
        ).astype(jnp.bfloat16)
        by_column = jnp.einsum(
            "mcil,iol->icmo", patch_block_slice, column_hot,
            preferred_element_type=jnp.float32,
        )
        channel_hot = (
            channel[:, None, :] == jnp.arange(channels, dtype=jnp.int32)[None, :, None]
        ).astype(jnp.float32)
        predicted = jnp.sum(by_column * channel_hot[:, :, None, :], axis=1)

        predicted_mean = jnp.mean(predicted, axis=1)
        perturb = predicted - predicted_mean[:, None, :]
        innovation = obs_values - predicted_mean
        gram_local = jnp.einsum(
            "pmo,po,pno->pmn", perturb, obs_prec, perturb, precision=highest
        )
        pull_vec = jnp.einsum(
            "pmo,po->pm", perturb, obs_prec * innovation, precision=highest
        )
        count = gram_local.shape[0]
        packed = jnp.concatenate(
            [gram_local.reshape(count, ensemble * ensemble), pull_vec], axis=1
        )
        for axis in GATHER_ORDER:
            packed = lax.all_gather(packed, axis, axis=0, tiled=False)
        packed = packed.reshape(-1, ensemble * ensemble + ensemble)
        total_patches = packed.shape[0]
        patch_ids = jnp.arange(total_patches, dtype=jnp.int32)
        matches = (neighbours[:, :, None] == patch_ids[None, None, :]).astype(jnp.float32)
        spread_weights = jnp.sum(loc_weight[:, :, None] * matches, axis=1)
        summed = jnp.einsum("pj,jf->pf", spread_weights, packed, precision=highest)
        gram_sum = summed[:, : ensemble * ensemble].reshape(count, ensemble, ensemble)
        pull_sum = summed[:, ensemble * ensemble :]
        identity = jnp.broadcast_to(
            jnp.eye(ensemble, dtype=jnp.float32), (height, ensemble, ensemble)
        )
        matrix = (ensemble - 1.0) * identity + gram_local + gram_sum
        pulled = pull_vec + pull_sum
        norm_scale = jnp.sqrt(jnp.sum(matrix * matrix, axis=(1, 2)))
        sqrt_iter = matrix / norm_scale[:, None, None]
        inverse_root = identity
        for sweep in range(NS_ITERS):
            half_step = 1.5 * identity - 0.5 * jnp.einsum(
                "pab,pbc->pac", inverse_root, sqrt_iter, precision=highest
            )
            sqrt_iter = jnp.einsum("pab,pbc->pac", sqrt_iter, half_step, precision=highest)
            inverse_root = jnp.einsum("pab,pbc->pac", half_step, inverse_root, precision=highest)
        once_applied = jnp.einsum("pab,pb->pa", inverse_root, pulled, precision=highest)
        mean_weight = (
            jnp.einsum("pab,pb->pa", inverse_root, once_applied, precision=highest)
            / norm_scale[:, None]
        )
        transform = (jnp.sqrt(ensemble - 1.0) / jnp.sqrt(norm_scale))[
            :, None, None
        ] * inverse_root + mean_weight[:, :, None]
        realization_grid = jnp.transpose(patch_block_slice, (2, 0, 1, 3)).reshape(
            height, ensemble, channels * patch_width
        )
        field = realization_grid.astype(jnp.float32)
        centre = jnp.mean(field, axis=1)
        spread = field - centre[:, None, :]
        analysed = centre[:, None, :] + jnp.einsum(
            "pkm,pkc->pmc", transform, spread, precision=highest
        )
        return analysed.reshape(height, ensemble, channels, patch_width).transpose(1, 2, 0, 3)

    return on_device


def solution(mesh):
    grp_size, band_size = mesh.devices.shape
    fine = Mesh(
        mesh.devices.reshape(grp_size // 2, 2, 2, band_size // 32 * 4, 4),
        GRP + BAND,
    )
    placed = (
        P(GRP, None, BAND, None),
        P(),
        P(),
        P(),
        P(),
        P(GRP + BAND, None),
        P(GRP + BAND, None),
        P(GRP + BAND, None),
        P(GRP + BAND, None),
        P(GRP + BAND, None),
    )
    return jax.shard_map(
        make_on_device(band_size),
        mesh=fine,
        in_specs=placed,
        out_specs=P(None, None, BAND, GRP),
        check_vma=False,
    )
```

```python
import jax
import jax.numpy as jnp
import numpy as np
from jax import lax
from jax.sharding import Mesh
from jax.sharding import PartitionSpec as P

NS_ITERS = 6

GRP = ("y_lo", "core")
BAND = ("y_hi", "x", "z")
GATHER_ORDER = ("z", "x", "y_hi", "core", "y_lo")


def shift_pairs(count, step):
    return [(i, i + step) for i in range(count) if 0 <= i + step < count]


def padded_2(cells, band_size, width):
    head = lax.slice_in_dim(cells, 0, width, axis=2)
    tail = lax.slice_in_dim(cells, cells.shape[2] - width, cells.shape[2], axis=2)
    return jnp.concatenate(
        [
            lax.ppermute(tail, BAND, shift_pairs(band_size, 1)),
            cells,
            lax.ppermute(head, BAND, shift_pairs(band_size, -1)),
        ],
        axis=2,
    )


def convolve(padded, kernel):
    wrapped = jnp.concatenate([padded[..., -1:], padded, padded[..., :1]], axis=-1)
    return lax.conv_general_dilated(
        wrapped,
        jnp.transpose(kernel, (2, 3, 0, 1)),
        window_strides=(1, 1),
        padding="VALID",
        dimension_numbers=("NCHW", "OIHW", "NCHW"),
        preferred_element_type=jnp.float32,
    )


def make_on_device(band_size):
    def on_device(
        prior_samples,
        conv1_weight,
        conv1_bias,
        conv2_weight,
        conv2_bias,
        obs_index,
        obs_values,
        obs_prec,
        neighbours,
        loc_weight,
    ):
        highest = lax.Precision.HIGHEST
        height = prior_samples.shape[2]
        padded = padded_2(prior_samples, band_size, height)
        hidden_fields = jax.nn.silu(
            convolve(padded, conv1_weight) + conv1_bias[None, :, None, None]
        ).astype(jnp.bfloat16)
        place = lax.axis_index(BAND)
        row_ids = jnp.arange(height + 2, dtype=jnp.int32)[None, None, :, None]
        outside = ((place == 0) & (row_ids == 0)) | (
            (place == band_size - 1) & (row_ids == height + 1)
        )
        extended = jnp.where(outside, jnp.zeros_like(hidden_fields), hidden_fields)
        predicted_samples = (
            prior_samples.astype(jnp.float32)
            + convolve(extended, conv2_weight)
            + conv2_bias[None, :, None, None]
        ).astype(jnp.bfloat16)
        patch_block_slice = lax.all_to_all(
            predicted_samples, GRP, split_axis=3, concat_axis=0, tiled=True
        )
        ensemble = patch_block_slice.shape[0]
        channels = patch_block_slice.shape[1]
        patch_width = patch_block_slice.shape[3]

        column = obs_index % patch_width
        channel = obs_index // patch_width
        column_hot = (
            column[:, :, None] == jnp.arange(patch_width, dtype=jnp.int32)[None, None, :]
        ).astype(jnp.bfloat16)
        by_column = jnp.einsum(
            "mcil,iol->icmo", patch_block_slice, column_hot,
            preferred_element_type=jnp.float32,
        )
        channel_hot = (
            channel[:, None, :] == jnp.arange(channels, dtype=jnp.int32)[None, :, None]
        ).astype(jnp.float32)
        predicted = jnp.sum(by_column * channel_hot[:, :, None, :], axis=1)

        predicted_mean = jnp.mean(predicted, axis=1)
        perturb = predicted - predicted_mean[:, None, :]
        innovation = obs_values - predicted_mean
        gram_local = jnp.einsum(
            "pmo,po,pno->pmn", perturb, obs_prec, perturb, precision=highest
        )
        pull_vec = jnp.einsum(
            "pmo,po->pm", perturb, obs_prec * innovation, precision=highest
        )
        count = gram_local.shape[0]
        packed = jnp.concatenate(
            [gram_local.reshape(count, ensemble * ensemble), pull_vec], axis=1
        )
        for axis in GATHER_ORDER:
            packed = lax.all_gather(packed, axis, axis=0, tiled=False)
        packed = packed.reshape(-1, ensemble * ensemble + ensemble)
        total_patches = packed.shape[0]
        patch_ids = jnp.arange(total_patches, dtype=jnp.int32)
        matches = (neighbours[:, :, None] == patch_ids[None, None, :]).astype(jnp.float32)
        spread_weights = jnp.sum(loc_weight[:, :, None] * matches, axis=1)
        summed = jnp.einsum("pj,jf->pf", spread_weights, packed, precision=highest)
        gram_sum = summed[:, : ensemble * ensemble].reshape(count, ensemble, ensemble)
        pull_sum = summed[:, ensemble * ensemble :]
        identity = jnp.broadcast_to(
            jnp.eye(ensemble, dtype=jnp.float32), (height, ensemble, ensemble)
        )
        matrix = (ensemble - 1.0) * identity + gram_local + gram_sum
        pulled = pull_vec + pull_sum
        norm_scale = jnp.sqrt(jnp.sum(matrix * matrix, axis=(1, 2)))
        sqrt_iter = matrix / norm_scale[:, None, None]
        inverse_root = identity
        for sweep in range(NS_ITERS):
            half_step = 1.5 * identity - 0.5 * jnp.einsum(
                "pab,pbc->pac", inverse_root, sqrt_iter, precision=highest
            )
            sqrt_iter = jnp.einsum("pab,pbc->pac", sqrt_iter, half_step, precision=highest)
            inverse_root = jnp.einsum("pab,pbc->pac", half_step, inverse_root, precision=highest)
        once_applied = jnp.einsum("pab,pb->pa", inverse_root, pulled, precision=highest)
        mean_weight = (
            jnp.einsum("pab,pb->pa", inverse_root, once_applied, precision=highest)
            / norm_scale[:, None]
        )
        transform = (jnp.sqrt(ensemble - 1.0) / jnp.sqrt(norm_scale))[
            :, None, None
        ] * inverse_root + mean_weight[:, :, None]
        realization_grid = jnp.transpose(patch_block_slice, (2, 0, 1, 3)).reshape(
            height, ensemble, channels * patch_width
        )
        field = realization_grid.astype(jnp.float32)
        centre = jnp.mean(field, axis=1)
        spread = field - centre[:, None, :]
        analysed = centre[:, None, :] + jnp.einsum(
            "pkm,pkc->pmc", transform, spread, precision=highest
        )
        return analysed.reshape(height, ensemble, channels, patch_width).transpose(1, 2, 0, 3)

    return on_device


def solution(mesh):
    grp_size, band_size = mesh.devices.shape
    fine = Mesh(
        mesh.devices.reshape(grp_size // 2, 2, 2, band_size // 32 * 4, 4),
        GRP + BAND,
    )
    placed = (
        P(GRP, None, BAND, None),
        P(),
        P(),
        P(),
        P(),
        P(GRP + BAND, None),
        P(GRP + BAND, None),
        P(GRP + BAND, None),
        P(GRP + BAND, None),
        P(GRP + BAND, None),
    )
    return jax.shard_map(
        make_on_device(band_size),
        mesh=fine,
        in_specs=placed,
        out_specs=P(None, None, BAND, GRP),
        check_vma=False,
    )
```

```python
import jax
import jax.numpy as jnp
import numpy as np
from jax import lax
from jax.sharding import Mesh
from jax.sharding import PartitionSpec as P

NS_ITERS = 6

GRP = ("y_lo", "core")
BAND = ("y_hi", "x", "z")
GATHER_ORDER = ("z", "x", "y_hi", "core", "y_lo")


def shift_pairs(count, step):
    return [(i, i + step) for i in range(count) if 0 <= i + step < count]


def padded_2(cells, band_size, width):
    head = lax.slice_in_dim(cells, 0, width, axis=2)
    tail = lax.slice_in_dim(cells, cells.shape[2] - width, cells.shape[2], axis=2)
    return jnp.concatenate(
        [
            lax.ppermute(tail, BAND, shift_pairs(band_size, 1)),
            cells,
            lax.ppermute(head, BAND, shift_pairs(band_size, -1)),
        ],
        axis=2,
    )


def convolve(padded, kernel):
    wrapped = jnp.concatenate([padded[..., -1:], padded, padded[..., :1]], axis=-1)
    return lax.conv_general_dilated(
        wrapped,
        jnp.transpose(kernel, (2, 3, 0, 1)),
        window_strides=(1, 1),
        padding="VALID",
        dimension_numbers=("NCHW", "OIHW", "NCHW"),
        preferred_element_type=jnp.float32,
    )


def make_on_device(band_size):
    def on_device(
        prior_samples,
        conv1_weight,
        conv1_bias,
        conv2_weight,
        conv2_bias,
        obs_index,
        obs_values,
        obs_prec,
        neighbours,
        loc_weight,
    ):
        highest = lax.Precision.HIGHEST
        height = prior_samples.shape[2]
        padded = padded_2(prior_samples, band_size, height)
        hidden_fields = jax.nn.silu(
            convolve(padded, conv1_weight) + conv1_bias[None, :, None, None]
        ).astype(jnp.bfloat16)
        place = lax.axis_index(BAND)
        row_ids = jnp.arange(height + 2, dtype=jnp.int32)[None, None, :, None]
        outside = ((place == 0) & (row_ids == 0)) | (
            (place == band_size - 1) & (row_ids == height + 1)
        )
        extended = jnp.where(outside, jnp.zeros_like(hidden_fields), hidden_fields)
        predicted_samples = (
            prior_samples.astype(jnp.float32)
            + convolve(extended, conv2_weight)
            + conv2_bias[None, :, None, None]
        ).astype(jnp.bfloat16)
        ensemble_part = predicted_samples.shape[0]
        channels = predicted_samples.shape[1]
        quarters = lax.psum(1, GRP)
        patch_width = predicted_samples.shape[3] // quarters
        row_index = lax.all_gather(obs_index, GRP, axis=0, tiled=False)
        column = row_index % patch_width
        channel = row_index // patch_width
        column_hot = (
            column[..., None] == jnp.arange(patch_width, dtype=jnp.int32)
        ).astype(jnp.bfloat16)
        by_column = jnp.einsum(
            "mciql,qiol->qicmo",
            predicted_samples.reshape(ensemble_part, channels, height, quarters, patch_width),
            column_hot,
            preferred_element_type=jnp.float32,
        )
        channel_hot = (
            channel[:, :, None, :] == jnp.arange(channels, dtype=jnp.int32)[None, None, :, None]
        ).astype(jnp.float32)
        own_members = jnp.sum(by_column * channel_hot[:, :, :, None, :], axis=2)
        predicted = lax.all_to_all(own_members, GRP, split_axis=0, concat_axis=2, tiled=True)[0]
        patch_block_slice = lax.all_to_all(
            predicted_samples, GRP, split_axis=3, concat_axis=0, tiled=True
        )
        ensemble = patch_block_slice.shape[0]
        predicted_mean = jnp.mean(predicted, axis=1)
        perturb = predicted - predicted_mean[:, None, :]
        innovation = obs_values - predicted_mean
        gram_local = jnp.einsum(
            "pmo,po,pno->pmn", perturb, obs_prec, perturb, precision=highest
        )
        pull_vec = jnp.einsum(
            "pmo,po->pm", perturb, obs_prec * innovation, precision=highest
        )
        count = gram_local.shape[0]
        packed = jnp.concatenate(
            [gram_local.reshape(count, ensemble * ensemble), pull_vec], axis=1
        )
        for axis in GATHER_ORDER:
            packed = lax.all_gather(packed, axis, axis=0, tiled=False)
        packed = packed.reshape(-1, ensemble * ensemble + ensemble)
        total_patches = packed.shape[0]
        patch_ids = jnp.arange(total_patches, dtype=jnp.int32)
        matches = (neighbours[:, :, None] == patch_ids[None, None, :]).astype(jnp.float32)
        spread_weights = jnp.sum(loc_weight[:, :, None] * matches, axis=1)
        summed = jnp.einsum("pj,jf->pf", spread_weights, packed, precision=highest)
        gram_sum = summed[:, : ensemble * ensemble].reshape(count, ensemble, ensemble)
        pull_sum = summed[:, ensemble * ensemble :]
        identity = jnp.broadcast_to(
            jnp.eye(ensemble, dtype=jnp.float32), (height, ensemble, ensemble)
        )
        matrix = (ensemble - 1.0) * identity + gram_local + gram_sum
        pulled = pull_vec + pull_sum
        norm_scale = jnp.sqrt(jnp.sum(matrix * matrix, axis=(1, 2)))
        sqrt_iter = matrix / norm_scale[:, None, None]
        inverse_root = identity
        for sweep in range(NS_ITERS):
            half_step = 1.5 * identity - 0.5 * jnp.einsum(
                "pab,pbc->pac", inverse_root, sqrt_iter, precision=highest
            )
            sqrt_iter = jnp.einsum("pab,pbc->pac", sqrt_iter, half_step, precision=highest)
            inverse_root = jnp.einsum("pab,pbc->pac", half_step, inverse_root, precision=highest)
        once_applied = jnp.einsum("pab,pb->pa", inverse_root, pulled, precision=highest)
        mean_weight = (
            jnp.einsum("pab,pb->pa", inverse_root, once_applied, precision=highest)
            / norm_scale[:, None]
        )
        transform = (jnp.sqrt(ensemble - 1.0) / jnp.sqrt(norm_scale))[
            :, None, None
        ] * inverse_root + mean_weight[:, :, None]
        realization_grid = jnp.transpose(patch_block_slice, (2, 0, 1, 3)).reshape(
            height, ensemble, channels * patch_width
        )
        field = realization_grid.astype(jnp.float32)
        centre = jnp.mean(field, axis=1)
        spread = field - centre[:, None, :]
        analysed = centre[:, None, :] + jnp.einsum(
            "pkm,pkc->pmc", transform, spread, precision=highest
        )
        return analysed.reshape(height, ensemble, channels, patch_width).transpose(1, 2, 0, 3)

    return on_device


def solution(mesh):
    grp_size, band_size = mesh.devices.shape
    fine = Mesh(
        mesh.devices.reshape(grp_size // 2, 2, 2, band_size // 32 * 4, 4),
        GRP + BAND,
    )
    placed = (
        P(GRP, None, BAND, None),
        P(),
        P(),
        P(),
        P(),
        P(GRP + BAND, None),
        P(GRP + BAND, None),
        P(GRP + BAND, None),
        P(GRP + BAND, None),
        P(GRP + BAND, None),
    )
    return jax.shard_map(
        make_on_device(band_size),
        mesh=fine,
        in_specs=placed,
        out_specs=P(None, None, BAND, GRP),
        check_vma=False,
    )
```

```python
import jax
import jax.numpy as jnp
import numpy as np
from jax import lax
from jax.sharding import Mesh
from jax.sharding import PartitionSpec as P

NS_ITERS = 6

GRP = ("y_lo", "core")
BAND = ("y_hi", "x", "z")
GATHER_ORDER = ("z", "x", "y_hi", "core", "y_lo")


def shift_pairs(count, step):
    return [(i, i + step) for i in range(count) if 0 <= i + step < count]


def padded_2(cells, band_size, width):
    head = lax.slice_in_dim(cells, 0, width, axis=2)
    tail = lax.slice_in_dim(cells, cells.shape[2] - width, cells.shape[2], axis=2)
    return jnp.concatenate(
        [
            lax.ppermute(tail, BAND, shift_pairs(band_size, 1)),
            cells,
            lax.ppermute(head, BAND, shift_pairs(band_size, -1)),
        ],
        axis=2,
    )


def convolve(padded, kernel):
    wrapped = jnp.concatenate([padded[..., -1:], padded, padded[..., :1]], axis=-1)
    return lax.conv_general_dilated(
        wrapped,
        jnp.transpose(kernel, (2, 3, 0, 1)),
        window_strides=(1, 1),
        padding="VALID",
        dimension_numbers=("NCHW", "OIHW", "NCHW"),
        preferred_element_type=jnp.float32,
    )


def make_on_device(band_size):
    def on_device(
        prior_samples,
        conv1_weight,
        conv1_bias,
        conv2_weight,
        conv2_bias,
        obs_index,
        obs_values,
        obs_prec,
        neighbours,
        loc_weight,
    ):
        highest = lax.Precision.HIGHEST
        height = prior_samples.shape[2]
        padded = padded_2(prior_samples, band_size, height)
        hidden_fields = jax.nn.silu(
            convolve(padded, conv1_weight) + conv1_bias[None, :, None, None]
        ).astype(jnp.bfloat16)
        place = lax.axis_index(BAND)
        row_ids = jnp.arange(height + 2, dtype=jnp.int32)[None, None, :, None]
        outside = ((place == 0) & (row_ids == 0)) | (
            (place == band_size - 1) & (row_ids == height + 1)
        )
        extended = jnp.where(outside, jnp.zeros_like(hidden_fields), hidden_fields)
        predicted_samples = (
            prior_samples.astype(jnp.float32)
            + convolve(extended, conv2_weight)
            + conv2_bias[None, :, None, None]
        ).astype(jnp.bfloat16)
        ensemble_part = predicted_samples.shape[0]
        channels = predicted_samples.shape[1]
        quarters = lax.psum(1, GRP)
        patch_width = predicted_samples.shape[3] // quarters
        row_index = lax.all_gather(obs_index, GRP, axis=0, tiled=False)
        column = row_index % patch_width
        channel = row_index // patch_width
        column_hot = (
            column[..., None] == jnp.arange(patch_width, dtype=jnp.int32)
        ).astype(jnp.bfloat16)
        by_column = jnp.einsum(
            "mciql,qiol->qicmo",
            predicted_samples.reshape(ensemble_part, channels, height, quarters, patch_width),
            column_hot,
            preferred_element_type=jnp.float32,
        )
        channel_hot = (
            channel[:, :, None, :] == jnp.arange(channels, dtype=jnp.int32)[None, None, :, None]
        ).astype(jnp.float32)
        own_members = jnp.sum(by_column * channel_hot[:, :, :, None, :], axis=2)
        predicted = lax.all_to_all(own_members, GRP, split_axis=0, concat_axis=2, tiled=True)[0]
        me = lax.axis_index(GRP)
        blocks = predicted_samples.reshape(ensemble_part, channels, height, quarters, patch_width)
        pieces = [lax.dynamic_index_in_dim(blocks, me, axis=3, keepdims=False)]
        for step in range(1, quarters):
            outgoing = lax.dynamic_index_in_dim(blocks, (me + step) % quarters, axis=3, keepdims=False)
            pieces.append(
                lax.ppermute(outgoing, GRP, [(j, (j + step) % quarters) for j in range(quarters)])
            )
        patch_block_slice = jnp.concatenate(pieces, axis=0)
        ensemble = patch_block_slice.shape[0]
        source_member = (
            ((me - jnp.arange(quarters, dtype=jnp.int32)) % quarters)[:, None] * ensemble_part
            + jnp.arange(ensemble_part, dtype=jnp.int32)[None, :]
        ).reshape(ensemble)
        predicted_mean = jnp.mean(predicted, axis=1)
        perturb = predicted - predicted_mean[:, None, :]
        innovation = obs_values - predicted_mean
        gram_local = jnp.einsum(
            "pmo,po,pno->pmn", perturb, obs_prec, perturb, precision=highest
        )
        pull_vec = jnp.einsum(
            "pmo,po->pm", perturb, obs_prec * innovation, precision=highest
        )
        count = gram_local.shape[0]
        packed = jnp.concatenate(
            [gram_local.reshape(count, ensemble * ensemble), pull_vec], axis=1
        )
        for axis in GATHER_ORDER:
            packed = lax.all_gather(packed, axis, axis=0, tiled=False)
        packed = packed.reshape(-1, ensemble * ensemble + ensemble)
        total_patches = packed.shape[0]
        patch_ids = jnp.arange(total_patches, dtype=jnp.int32)
        matches = (neighbours[:, :, None] == patch_ids[None, None, :]).astype(jnp.float32)
        spread_weights = jnp.sum(loc_weight[:, :, None] * matches, axis=1)
        summed = jnp.einsum("pj,jf->pf", spread_weights, packed, precision=highest)
        gram_sum = summed[:, : ensemble * ensemble].reshape(count, ensemble, ensemble)
        pull_sum = summed[:, ensemble * ensemble :]
        identity = jnp.broadcast_to(
            jnp.eye(ensemble, dtype=jnp.float32), (height, ensemble, ensemble)
        )
        matrix = (ensemble - 1.0) * identity + gram_local + gram_sum
        pulled = pull_vec + pull_sum
        norm_scale = jnp.sqrt(jnp.sum(matrix * matrix, axis=(1, 2)))
        sqrt_iter = matrix / norm_scale[:, None, None]
        inverse_root = identity
        for sweep in range(NS_ITERS):
            half_step = 1.5 * identity - 0.5 * jnp.einsum(
                "pab,pbc->pac", inverse_root, sqrt_iter, precision=highest
            )
            sqrt_iter = jnp.einsum("pab,pbc->pac", sqrt_iter, half_step, precision=highest)
            inverse_root = jnp.einsum("pab,pbc->pac", half_step, inverse_root, precision=highest)
        once_applied = jnp.einsum("pab,pb->pa", inverse_root, pulled, precision=highest)
        mean_weight = (
            jnp.einsum("pab,pb->pa", inverse_root, once_applied, precision=highest)
            / norm_scale[:, None]
        )
        transform = (jnp.sqrt(ensemble - 1.0) / jnp.sqrt(norm_scale))[
            :, None, None
        ] * inverse_root + mean_weight[:, :, None]
        weights = transform + (1.0 - jnp.sum(transform, axis=1, keepdims=True)) / ensemble
        weights = jnp.take(weights, source_member, axis=1)
        patch_of = jnp.arange(height, dtype=jnp.int32)
        spread_out = jnp.where(
            (patch_of[:, None] == patch_of[None, :])[None, :, None, :, None],
            patch_block_slice.astype(jnp.float32)[:, None],
            0.0,
        )
        analysed = jnp.einsum(
            "ikm,kicjl->mcjl", weights, spread_out, precision=highest
        )
        return analysed

    return on_device


def solution(mesh):
    grp_size, band_size = mesh.devices.shape
    fine = Mesh(
        mesh.devices.reshape(grp_size // 2, 2, 2, band_size // 32 * 4, 4),
        GRP + BAND,
    )
    placed = (
        P(GRP, None, BAND, None),
        P(),
        P(),
        P(),
        P(),
        P(GRP + BAND, None),
        P(GRP + BAND, None),
        P(GRP + BAND, None),
        P(GRP + BAND, None),
        P(GRP + BAND, None),
    )
    return jax.shard_map(
        make_on_device(band_size),
        mesh=fine,
        in_specs=placed,
        out_specs=P(None, None, BAND, GRP),
        check_vma=False,
    )
```

```python
import jax
import jax.numpy as jnp
import numpy as np
from jax import lax
from jax.sharding import Mesh
from jax.sharding import PartitionSpec as P

NS_ITERS = 6

GRP = ("y_lo", "core")
BAND = ("y_hi", "x", "z")
GATHER_ORDER = ("z", "x", "y_hi", "y_lo", "core")


def shift_pairs(count, step):
    return [(i, i + step) for i in range(count) if 0 <= i + step < count]


def padded_2(cells, band_size, width):
    head = lax.slice_in_dim(cells, 0, width, axis=2)
    tail = lax.slice_in_dim(cells, cells.shape[2] - width, cells.shape[2], axis=2)
    return jnp.concatenate(
        [
            lax.ppermute(tail, BAND, shift_pairs(band_size, 1)),
            cells,
            lax.ppermute(head, BAND, shift_pairs(band_size, -1)),
        ],
        axis=2,
    )


def convolve(padded, kernel):
    wrapped = jnp.concatenate([padded[..., -1:], padded, padded[..., :1]], axis=-1)
    return lax.conv_general_dilated(
        wrapped,
        jnp.transpose(kernel, (2, 3, 0, 1)),
        window_strides=(1, 1),
        padding="VALID",
        dimension_numbers=("NCHW", "OIHW", "NCHW"),
        preferred_element_type=jnp.float32,
    )


def make_on_device(band_size):
    def on_device(
        prior_samples,
        conv1_weight,
        conv1_bias,
        conv2_weight,
        conv2_bias,
        obs_index,
        obs_values,
        obs_prec,
        neighbours,
        loc_weight,
    ):
        highest = lax.Precision.HIGHEST
        height = prior_samples.shape[2]
        padded = padded_2(prior_samples, band_size, height)
        hidden_fields = jax.nn.silu(
            convolve(padded, conv1_weight) + conv1_bias[None, :, None, None]
        ).astype(jnp.bfloat16)
        place = lax.axis_index(BAND)
        row_ids = jnp.arange(height + 2, dtype=jnp.int32)[None, None, :, None]
        outside = ((place == 0) & (row_ids == 0)) | (
            (place == band_size - 1) & (row_ids == height + 1)
        )
        extended = jnp.where(outside, jnp.zeros_like(hidden_fields), hidden_fields)
        predicted_samples = (
            prior_samples.astype(jnp.float32)
            + convolve(extended, conv2_weight)
            + conv2_bias[None, :, None, None]
        ).astype(jnp.bfloat16)
        ensemble_part = predicted_samples.shape[0]
        channels = predicted_samples.shape[1]
        quarters = lax.psum(1, GRP)
        patch_width = predicted_samples.shape[3] // quarters
        row_index = lax.all_gather(obs_index, GRP, axis=0, tiled=False)
        column = row_index % patch_width
        channel = row_index // patch_width
        column_hot = (
            column[..., None] == jnp.arange(patch_width, dtype=jnp.int32)
        ).astype(jnp.bfloat16)
        by_column = jnp.einsum(
            "mciql,qiol->qicmo",
            predicted_samples.reshape(ensemble_part, channels, height, quarters, patch_width),
            column_hot,
            preferred_element_type=jnp.float32,
        )
        channel_hot = (
            channel[:, :, None, :] == jnp.arange(channels, dtype=jnp.int32)[None, None, :, None]
        ).astype(jnp.float32)
        own_members = jnp.sum(by_column * channel_hot[:, :, :, None, :], axis=2)
        predicted = lax.all_to_all(own_members, GRP, split_axis=0, concat_axis=2, tiled=True)[0]
        me = lax.axis_index(GRP)
        blocks = predicted_samples.reshape(ensemble_part, channels, height, quarters, patch_width)
        pieces = [lax.dynamic_index_in_dim(blocks, me, axis=3, keepdims=False)]
        for step in range(1, quarters):
            outgoing = lax.dynamic_index_in_dim(blocks, (me + step) % quarters, axis=3, keepdims=False)
            pieces.append(
                lax.ppermute(outgoing, GRP, [(j, (j + step) % quarters) for j in range(quarters)])
            )
        patch_block_slice = jnp.concatenate(pieces, axis=0)
        ensemble = patch_block_slice.shape[0]
        source_member = (
            ((me - jnp.arange(quarters, dtype=jnp.int32)) % quarters)[:, None] * ensemble_part
            + jnp.arange(ensemble_part, dtype=jnp.int32)[None, :]
        ).reshape(ensemble)
        predicted_mean = jnp.mean(predicted, axis=1)
        perturb = predicted - predicted_mean[:, None, :]
        innovation = obs_values - predicted_mean
        gram_local = jnp.einsum(
            "pmo,po,pno->pmn", perturb, obs_prec, perturb, precision=highest
        )
        pull_vec = jnp.einsum(
            "pmo,po->pm", perturb, obs_prec * innovation, precision=highest
        )
        count = gram_local.shape[0]
        packed = jnp.concatenate(
            [gram_local.reshape(count, ensemble * ensemble), pull_vec], axis=1
        )
        for axis in GATHER_ORDER:
            packed = lax.all_gather(packed, axis, axis=0, tiled=False)
        packed = packed.reshape(-1, ensemble * ensemble + ensemble)
        total_patches = packed.shape[0]
        quarter_patches = total_patches // 4
        gathered_row = (
            (neighbours // quarter_patches) % 2 * (2 * quarter_patches)
            + neighbours // (2 * quarter_patches) * quarter_patches
            + neighbours % quarter_patches
        )
        patch_ids = jnp.arange(total_patches, dtype=jnp.int32)
        matches = (gathered_row[:, :, None] == patch_ids[None, None, :]).astype(jnp.float32)
        spread_weights = jnp.sum(loc_weight[:, :, None] * matches, axis=1)
        summed = jnp.einsum("pj,jf->pf", spread_weights, packed, precision=highest)
        gram_sum = summed[:, : ensemble * ensemble].reshape(count, ensemble, ensemble)
        pull_sum = summed[:, ensemble * ensemble :]
        identity = jnp.broadcast_to(
            jnp.eye(ensemble, dtype=jnp.float32), (height, ensemble, ensemble)
        )
        matrix = (ensemble - 1.0) * identity + gram_local + gram_sum
        pulled = pull_vec + pull_sum
        norm_scale = jnp.sqrt(jnp.sum(matrix * matrix, axis=(1, 2)))
        sqrt_iter = matrix / norm_scale[:, None, None]
        inverse_root = identity
        for sweep in range(NS_ITERS):
            half_step = 1.5 * identity - 0.5 * jnp.einsum(
                "pab,pbc->pac", inverse_root, sqrt_iter, precision=highest
            )
            sqrt_iter = jnp.einsum("pab,pbc->pac", sqrt_iter, half_step, precision=highest)
            inverse_root = jnp.einsum("pab,pbc->pac", half_step, inverse_root, precision=highest)
        once_applied = jnp.einsum("pab,pb->pa", inverse_root, pulled, precision=highest)
        mean_weight = (
            jnp.einsum("pab,pb->pa", inverse_root, once_applied, precision=highest)
            / norm_scale[:, None]
        )
        transform = (jnp.sqrt(ensemble - 1.0) / jnp.sqrt(norm_scale))[
            :, None, None
        ] * inverse_root + mean_weight[:, :, None]
        weights = transform + (1.0 - jnp.sum(transform, axis=1, keepdims=True)) / ensemble
        weights = jnp.take(weights, source_member, axis=1)
        patch_of = jnp.arange(height, dtype=jnp.int32)
        spread_out = jnp.where(
            (patch_of[:, None] == patch_of[None, :])[None, :, None, :, None],
            patch_block_slice.astype(jnp.float32)[:, None],
            0.0,
        )
        analysed = jnp.einsum(
            "ikm,kicjl->mcjl", weights, spread_out, precision=highest
        )
        return analysed

    return on_device


def solution(mesh):
    grp_size, band_size = mesh.devices.shape
    fine = Mesh(
        mesh.devices.reshape(grp_size // 2, 2, 2, band_size // 32 * 4, 4),
        GRP + BAND,
    )
    placed = (
        P(GRP, None, BAND, None),
        P(),
        P(),
        P(),
        P(),
        P(GRP + BAND, None),
        P(GRP + BAND, None),
        P(GRP + BAND, None),
        P(GRP + BAND, None),
        P(GRP + BAND, None),
    )
    return jax.shard_map(
        make_on_device(band_size),
        mesh=fine,
        in_specs=placed,
        out_specs=P(None, None, BAND, GRP),
        check_vma=False,
    )
```

```python
import jax
import jax.numpy as jnp
import numpy as np
from jax import lax
from jax.experimental.layout import Layout, with_layout_constraint
from jax.sharding import Mesh
from jax.sharding import PartitionSpec as P

NS_ITERS = 6

GRP = ("y_lo", "core")
BAND = ("y_hi", "x", "z")
GATHER_ORDER = ("z", "x", "y_hi", "y_lo", "core")


def shift_pairs(count, step):
    return [(i, i + step) for i in range(count) if 0 <= i + step < count]


def padded_2(cells, band_size):
    return jnp.concatenate(
        [
            lax.ppermute(cells, BAND, shift_pairs(band_size, 1)),
            cells,
            lax.ppermute(cells, BAND, shift_pairs(band_size, -1)),
        ],
        axis=0,
    )


def convolve(padded, kernel):
    wrapped = jnp.concatenate([padded[:, -1:], padded, padded[:, :1]], axis=1)
    return lax.conv_general_dilated(
        wrapped,
        kernel,
        window_strides=(1, 1),
        padding="VALID",
        dimension_numbers=("HWNC", "HWOI", "HWNC"),
        preferred_element_type=jnp.float32,
    )


def make_on_device(band_size):
    def on_device(
        prior_samples,
        conv1_weight,
        conv1_bias,
        conv2_weight,
        conv2_bias,
        obs_index,
        obs_values,
        obs_prec,
        neighbours,
        loc_weight,
    ):
        highest = lax.Precision.HIGHEST
        rows_first = prior_samples
        height = rows_first.shape[0]
        padded = padded_2(rows_first, band_size)
        hidden_fields = jax.nn.silu(
            convolve(padded, conv1_weight) + conv1_bias
        ).astype(jnp.bfloat16)
        place = lax.axis_index(BAND)
        row_ids = jnp.arange(height + 2, dtype=jnp.int32)[:, None, None, None]
        outside = ((place == 0) & (row_ids == 0)) | (
            (place == band_size - 1) & (row_ids == height + 1)
        )
        extended = jnp.where(outside, jnp.zeros_like(hidden_fields), hidden_fields)
        forecast = (
            rows_first.astype(jnp.float32)
            + convolve(extended, conv2_weight)
            + conv2_bias
        ).astype(jnp.bfloat16)
        ensemble_part = forecast.shape[2]
        channels = forecast.shape[3]
        quarters = lax.psum(1, GRP)
        patch_width = forecast.shape[1] // quarters
        blocks = forecast.reshape(height, quarters, patch_width, ensemble_part, channels)
        row_index = lax.all_gather(obs_index, GRP, axis=0, tiled=False)
        column = row_index % patch_width
        channel = row_index // patch_width
        column_hot = (
            column[..., None] == jnp.arange(patch_width, dtype=jnp.int32)
        ).astype(jnp.bfloat16)
        by_column = jnp.einsum(
            "iqlmc,qiol->qicmo",
            blocks,
            column_hot,
            preferred_element_type=jnp.float32,
        )
        channel_hot = (
            channel[:, :, None, :] == jnp.arange(channels, dtype=jnp.int32)[None, None, :, None]
        ).astype(jnp.float32)
        own_members = jnp.sum(by_column * channel_hot[:, :, :, None, :], axis=2)
        predicted = lax.all_to_all(own_members, GRP, split_axis=0, concat_axis=2, tiled=True)[0]
        me = lax.axis_index(GRP)
        pieces = [lax.dynamic_index_in_dim(blocks, me, axis=1, keepdims=False)]
        for step in range(1, quarters):
            outgoing = lax.dynamic_index_in_dim(blocks, (me + step) % quarters, axis=1, keepdims=False)
            pieces.append(
                lax.ppermute(outgoing, GRP, [(j, (j + step) % quarters) for j in range(quarters)])
            )
        patch_block_slice = jnp.stack(pieces, axis=0)
        ensemble = quarters * ensemble_part
        source_member = (
            ((me - jnp.arange(quarters, dtype=jnp.int32)) % quarters)[:, None] * ensemble_part
            + jnp.arange(ensemble_part, dtype=jnp.int32)[None, :]
        ).reshape(ensemble)
        predicted_mean = jnp.mean(predicted, axis=1)
        perturb = predicted - predicted_mean[:, None, :]
        innovation = obs_values - predicted_mean
        gram_local = jnp.einsum(
            "pmo,po,pno->pmn", perturb, obs_prec, perturb, precision=highest
        )
        pull_vec = jnp.einsum(
            "pmo,po->pm", perturb, obs_prec * innovation, precision=highest
        )
        count = gram_local.shape[0]
        packed = jnp.concatenate(
            [gram_local.reshape(count, ensemble * ensemble), pull_vec], axis=1
        )
        for axis in GATHER_ORDER:
            packed = lax.all_gather(packed, axis, axis=0, tiled=False)
        packed = packed.reshape(-1, ensemble * ensemble + ensemble)
        total_patches = packed.shape[0]
        quarter_patches = total_patches // 4
        gathered_row = (
            (neighbours // quarter_patches) % 2 * (2 * quarter_patches)
            + neighbours // (2 * quarter_patches) * quarter_patches
            + neighbours % quarter_patches
        )
        patch_ids = jnp.arange(total_patches, dtype=jnp.int32)
        matches = (gathered_row[:, :, None] == patch_ids[None, None, :]).astype(jnp.float32)
        spread_weights = jnp.sum(loc_weight[:, :, None] * matches, axis=1)
        summed = jnp.einsum("pj,jf->pf", spread_weights, packed, precision=highest)
        gram_sum = summed[:, : ensemble * ensemble].reshape(count, ensemble, ensemble)
        pull_sum = summed[:, ensemble * ensemble :]
        identity = jnp.broadcast_to(
            jnp.eye(ensemble, dtype=jnp.float32), (height, ensemble, ensemble)
        )
        matrix = (ensemble - 1.0) * identity + gram_local + gram_sum
        pulled = pull_vec + pull_sum
        norm_scale = jnp.sqrt(jnp.sum(matrix * matrix, axis=(1, 2)))
        sqrt_iter = matrix / norm_scale[:, None, None]
        inverse_root = identity
        for sweep in range(NS_ITERS):
            half_step = 1.5 * identity - 0.5 * jnp.einsum(
                "pab,pbc->pac", inverse_root, sqrt_iter, precision=highest
            )
            sqrt_iter = jnp.einsum("pab,pbc->pac", sqrt_iter, half_step, precision=highest)
            inverse_root = jnp.einsum("pab,pbc->pac", half_step, inverse_root, precision=highest)
        once_applied = jnp.einsum("pab,pb->pa", inverse_root, pulled, precision=highest)
        mean_weight = (
            jnp.einsum("pab,pb->pa", inverse_root, once_applied, precision=highest)
            / norm_scale[:, None]
        )
        transform = (jnp.sqrt(ensemble - 1.0) / jnp.sqrt(norm_scale))[
            :, None, None
        ] * inverse_root + mean_weight[:, :, None]
        weights = transform + (1.0 - jnp.sum(transform, axis=1, keepdims=True)) / ensemble
        weights = jnp.take(weights, source_member, axis=1).reshape(
            height, quarters, ensemble_part, ensemble
        )
        patch_of = jnp.arange(height, dtype=jnp.int32)
        spread_out = jnp.where(
            (patch_of[:, None] == patch_of[None, :])[None, :, :, None, None, None],
            patch_block_slice.astype(jnp.float32)[:, None],
            0.0,
        )
        analysed = jnp.einsum(
            "ajnm,jailnc->mcil", weights, spread_out, precision=highest
        )
        return analysed

    return on_device


def solution(mesh):
    grp_size, band_size = mesh.devices.shape
    fine = Mesh(
        mesh.devices.reshape(grp_size // 2, 2, 2, band_size // 32 * 4, 4),
        GRP + BAND,
    )
    placed = (
        P(BAND, None, GRP, None),
        P(),
        P(),
        P(),
        P(),
        P(GRP + BAND, None),
        P(GRP + BAND, None),
        P(GRP + BAND, None),
        P(GRP + BAND, None),
        P(GRP + BAND, None),
    )
    mapped = jax.shard_map(
        make_on_device(band_size),
        mesh=fine,
        in_specs=placed,
        out_specs=P(None, None, BAND, GRP),
        check_vma=False,
    )

    def run(prior_samples, *rest):
        rows_first = with_layout_constraint(
            jnp.transpose(prior_samples, (2, 3, 0, 1)), Layout((0, 1, 2, 3))
        )
        return mapped(rows_first, *rest)

    return run
```

```python
import jax
import jax.numpy as jnp
import numpy as np
from jax import lax
from jax.experimental.layout import Layout, with_layout_constraint
from jax.sharding import Mesh
from jax.sharding import PartitionSpec as P

NS_ITERS = 6

GRP = ("y_lo", "core")
BAND = ("y_hi", "x", "z")


def shift_pairs(count, step):
    return [(i, i + step) for i in range(count) if 0 <= i + step < count]


def padded_2(cells, band_size):
    return jnp.concatenate(
        [
            lax.ppermute(cells, BAND, shift_pairs(band_size, 1)),
            cells,
            lax.ppermute(cells, BAND, shift_pairs(band_size, -1)),
        ],
        axis=0,
    )


def convolve(padded, kernel):
    wrapped = jnp.concatenate([padded[:, -1:], padded, padded[:, :1]], axis=1)
    return lax.conv_general_dilated(
        wrapped,
        kernel,
        window_strides=(1, 1),
        padding="VALID",
        dimension_numbers=("HWNC", "HWOI", "HWNC"),
        preferred_element_type=jnp.float32,
    )


def make_on_device(band_size):
    def on_device(
        prior_samples,
        conv1_weight,
        conv1_bias,
        conv2_weight,
        conv2_bias,
        obs_index,
        obs_values,
        obs_prec,
        neighbours,
        loc_weight,
    ):
        highest = lax.Precision.HIGHEST
        rows_first = prior_samples
        height = rows_first.shape[0]
        padded = padded_2(rows_first, band_size)
        hidden_fields = jax.nn.silu(
            convolve(padded, conv1_weight) + conv1_bias
        ).astype(jnp.bfloat16)
        place = lax.axis_index(BAND)
        row_ids = jnp.arange(height + 2, dtype=jnp.int32)[:, None, None, None]
        outside = ((place == 0) & (row_ids == 0)) | (
            (place == band_size - 1) & (row_ids == height + 1)
        )
        extended = jnp.where(outside, jnp.zeros_like(hidden_fields), hidden_fields)
        forecast = (
            rows_first.astype(jnp.float32)
            + convolve(extended, conv2_weight)
            + conv2_bias
        ).astype(jnp.bfloat16)
        ensemble_part = forecast.shape[2]
        channels = forecast.shape[3]
        quarters = lax.psum(1, GRP)
        patch_width = forecast.shape[1] // quarters
        blocks = forecast.reshape(height, quarters, patch_width, ensemble_part, channels)
        row_index = lax.all_gather(obs_index, GRP, axis=0, tiled=False)
        column = row_index % patch_width
        channel = row_index // patch_width
        column_hot = (
            column[..., None] == jnp.arange(patch_width, dtype=jnp.int32)
        ).astype(jnp.bfloat16)
        by_column = jnp.einsum(
            "iqlmc,qiol->qicmo",
            blocks,
            column_hot,
            preferred_element_type=jnp.float32,
        )
        channel_hot = (
            channel[:, :, None, :] == jnp.arange(channels, dtype=jnp.int32)[None, None, :, None]
        ).astype(jnp.float32)
        own_members = jnp.sum(by_column * channel_hot[:, :, :, None, :], axis=2)
        predicted = lax.all_to_all(own_members, GRP, split_axis=0, concat_axis=2, tiled=True)[0]
        me = lax.axis_index(GRP)
        pieces = [lax.dynamic_index_in_dim(blocks, me, axis=1, keepdims=False)]
        for step in range(1, quarters):
            outgoing = lax.dynamic_index_in_dim(blocks, (me + step) % quarters, axis=1, keepdims=False)
            pieces.append(
                lax.ppermute(outgoing, GRP, [(j, (j + step) % quarters) for j in range(quarters)])
            )
        patch_block_slice = jnp.stack(pieces, axis=0)
        ensemble = quarters * ensemble_part
        source_member = (
            ((me - jnp.arange(quarters, dtype=jnp.int32)) % quarters)[:, None] * ensemble_part
            + jnp.arange(ensemble_part, dtype=jnp.int32)[None, :]
        ).reshape(ensemble)
        predicted_mean = jnp.mean(predicted, axis=1)
        perturb = predicted - predicted_mean[:, None, :]
        innovation = obs_values - predicted_mean
        gram_local = jnp.einsum(
            "pmo,po,pno->pmn", perturb, obs_prec, perturb, precision=highest
        )
        pull_vec = jnp.einsum(
            "pmo,po->pm", perturb, obs_prec * innovation, precision=highest
        )
        count = gram_local.shape[0]
        packed = jnp.concatenate(
            [gram_local.reshape(count, ensemble * ensemble), pull_vec], axis=1
        )
        devices = lax.psum(1, GRP + BAND)
        packed = lax.all_to_all(
            jnp.broadcast_to(packed[None], (devices,) + packed.shape),
            GRP + BAND, split_axis=0, concat_axis=0, tiled=True,
        )
        packed = packed.reshape(-1, ensemble * ensemble + ensemble)
        total_patches = packed.shape[0]
        patch_ids = jnp.arange(total_patches, dtype=jnp.int32)
        matches = (neighbours[:, :, None] == patch_ids[None, None, :]).astype(jnp.float32)
        spread_weights = jnp.sum(loc_weight[:, :, None] * matches, axis=1)
        summed = jnp.einsum("pj,jf->pf", spread_weights, packed, precision=highest)
        gram_sum = summed[:, : ensemble * ensemble].reshape(count, ensemble, ensemble)
        pull_sum = summed[:, ensemble * ensemble :]
        identity = jnp.broadcast_to(
            jnp.eye(ensemble, dtype=jnp.float32), (height, ensemble, ensemble)
        )
        matrix = (ensemble - 1.0) * identity + gram_local + gram_sum
        pulled = pull_vec + pull_sum
        norm_scale = jnp.sqrt(jnp.sum(matrix * matrix, axis=(1, 2)))
        sqrt_iter = matrix / norm_scale[:, None, None]
        inverse_root = identity
        for sweep in range(NS_ITERS):
            half_step = 1.5 * identity - 0.5 * jnp.einsum(
                "pab,pbc->pac", inverse_root, sqrt_iter, precision=highest
            )
            sqrt_iter = jnp.einsum("pab,pbc->pac", sqrt_iter, half_step, precision=highest)
            inverse_root = jnp.einsum("pab,pbc->pac", half_step, inverse_root, precision=highest)
        once_applied = jnp.einsum("pab,pb->pa", inverse_root, pulled, precision=highest)
        mean_weight = (
            jnp.einsum("pab,pb->pa", inverse_root, once_applied, precision=highest)
            / norm_scale[:, None]
        )
        transform = (jnp.sqrt(ensemble - 1.0) / jnp.sqrt(norm_scale))[
            :, None, None
        ] * inverse_root + mean_weight[:, :, None]
        weights = transform + (1.0 - jnp.sum(transform, axis=1, keepdims=True)) / ensemble
        weights = jnp.take(weights, source_member, axis=1).reshape(
            height, quarters, ensemble_part, ensemble
        )
        patch_of = jnp.arange(height, dtype=jnp.int32)
        spread_out = jnp.where(
            (patch_of[:, None] == patch_of[None, :])[None, :, :, None, None, None],
            patch_block_slice.astype(jnp.float32)[:, None],
            0.0,
        )
        analysed = jnp.einsum(
            "ajnm,jailnc->mcil", weights, spread_out, precision=highest
        )
        return analysed

    return on_device


def solution(mesh):
    grp_size, band_size = mesh.devices.shape
    fine = Mesh(
        mesh.devices.reshape(grp_size // 2, 2, 2, band_size // 32 * 4, 4),
        GRP + BAND,
    )
    placed = (
        P(BAND, None, GRP, None),
        P(),
        P(),
        P(),
        P(),
        P(GRP + BAND, None),
        P(GRP + BAND, None),
        P(GRP + BAND, None),
        P(GRP + BAND, None),
        P(GRP + BAND, None),
    )
    mapped = jax.shard_map(
        make_on_device(band_size),
        mesh=fine,
        in_specs=placed,
        out_specs=P(None, None, BAND, GRP),
        check_vma=False,
    )

    def run(prior_samples, *rest):
        rows_first = with_layout_constraint(
            jnp.transpose(prior_samples, (2, 3, 0, 1)), Layout((0, 1, 2, 3))
        )
        return mapped(rows_first, *rest)

    return run
```

```python
import jax
import jax.numpy as jnp
import numpy as np
from jax import lax
from jax.experimental.layout import Layout, with_layout_constraint
from jax.sharding import Mesh
from jax.sharding import PartitionSpec as P

NS_ITERS = 6

GRP = ("y_lo", "core")
BAND = ("y_hi", "x", "z")


def shift_pairs(count, step):
    return [(i, i + step) for i in range(count) if 0 <= i + step < count]


def padded_2(cells, band_size):
    return jnp.concatenate(
        [
            lax.ppermute(cells, BAND, shift_pairs(band_size, 1)),
            cells,
            lax.ppermute(cells, BAND, shift_pairs(band_size, -1)),
        ],
        axis=0,
    )


def convolve(padded, kernel):
    wrapped = jnp.concatenate([padded[:, -1:], padded, padded[:, :1]], axis=1)
    return lax.conv_general_dilated(
        wrapped,
        kernel,
        window_strides=(1, 1),
        padding="VALID",
        dimension_numbers=("HWNC", "HWOI", "HWNC"),
        preferred_element_type=jnp.float32,
    )


def convolve_stacked(padded, kernel):
    stacked = jnp.concatenate(
        [jnp.roll(padded, 1, axis=1), padded, jnp.roll(padded, -1, axis=1)], axis=3
    )
    rows_kernel = jnp.transpose(kernel, (0, 2, 1, 3)).reshape(
        kernel.shape[0], 1, kernel.shape[2], kernel.shape[1] * kernel.shape[3]
    )
    return lax.conv_general_dilated(
        stacked,
        rows_kernel,
        window_strides=(1, 1),
        padding="VALID",
        dimension_numbers=("HWNC", "HWOI", "HWNC"),
        preferred_element_type=jnp.float32,
    )


def make_on_device(band_size):
    def on_device(
        prior_samples,
        conv1_weight,
        conv1_bias,
        conv2_weight,
        conv2_bias,
        obs_index,
        obs_values,
        obs_prec,
        neighbours,
        loc_weight,
    ):
        highest = lax.Precision.HIGHEST
        rows_first = prior_samples
        height = rows_first.shape[0]
        padded = padded_2(rows_first, band_size)
        hidden_fields = jax.nn.silu(
            convolve_stacked(padded, conv1_weight) + conv1_bias
        ).astype(jnp.bfloat16)
        place = lax.axis_index(BAND)
        row_ids = jnp.arange(height + 2, dtype=jnp.int32)[:, None, None, None]
        outside = ((place == 0) & (row_ids == 0)) | (
            (place == band_size - 1) & (row_ids == height + 1)
        )
        extended = jnp.where(outside, jnp.zeros_like(hidden_fields), hidden_fields)
        forecast = (
            rows_first.astype(jnp.float32)
            + convolve(extended, conv2_weight)
            + conv2_bias
        ).astype(jnp.bfloat16)
        ensemble_part = forecast.shape[2]
        channels = forecast.shape[3]
        quarters = lax.psum(1, GRP)
        patch_width = forecast.shape[1] // quarters
        blocks = forecast.reshape(height, quarters, patch_width, ensemble_part, channels)
        row_index = lax.all_gather(obs_index, GRP, axis=0, tiled=False)
        column = row_index % patch_width
        channel = row_index // patch_width
        column_hot = (
            column[..., None] == jnp.arange(patch_width, dtype=jnp.int32)
        ).astype(jnp.bfloat16)
        by_column = jnp.einsum(
            "iqlmc,qiol->qicmo",
            blocks,
            column_hot,
            preferred_element_type=jnp.float32,
        )
        channel_hot = (
            channel[:, :, None, :] == jnp.arange(channels, dtype=jnp.int32)[None, None, :, None]
        ).astype(jnp.float32)
        own_members = jnp.sum(by_column * channel_hot[:, :, :, None, :], axis=2)
        predicted = lax.all_to_all(own_members, GRP, split_axis=0, concat_axis=2, tiled=True)[0]
        me = lax.axis_index(GRP)
        pieces = [lax.dynamic_index_in_dim(blocks, me, axis=1, keepdims=False)]
        for step in range(1, quarters):
            outgoing = lax.dynamic_index_in_dim(blocks, (me + step) % quarters, axis=1, keepdims=False)
            pieces.append(
                lax.ppermute(outgoing, GRP, [(j, (j + step) % quarters) for j in range(quarters)])
            )
        patch_block_slice = jnp.stack(pieces, axis=0)
        ensemble = quarters * ensemble_part
        source_member = (
            ((me - jnp.arange(quarters, dtype=jnp.int32)) % quarters)[:, None] * ensemble_part
            + jnp.arange(ensemble_part, dtype=jnp.int32)[None, :]
        ).reshape(ensemble)
        predicted_mean = jnp.mean(predicted, axis=1)
        perturb = predicted - predicted_mean[:, None, :]
        innovation = obs_values - predicted_mean
        gram_local = jnp.einsum(
            "pmo,po,pno->pmn", perturb, obs_prec, perturb, precision=highest
        )
        pull_vec = jnp.einsum(
            "pmo,po->pm", perturb, obs_prec * innovation, precision=highest
        )
        count = gram_local.shape[0]
        packed = jnp.concatenate(
            [gram_local.reshape(count, ensemble * ensemble), pull_vec], axis=1
        )
        devices = lax.psum(1, GRP + BAND)
        packed = lax.all_to_all(
            jnp.broadcast_to(packed[None], (devices,) + packed.shape),
            GRP + BAND, split_axis=0, concat_axis=0, tiled=True,
        )
        packed = packed.reshape(-1, ensemble * ensemble + ensemble)
        total_patches = packed.shape[0]
        patch_ids = jnp.arange(total_patches, dtype=jnp.int32)
        matches = (neighbours[:, :, None] == patch_ids[None, None, :]).astype(jnp.float32)
        spread_weights = jnp.sum(loc_weight[:, :, None] * matches, axis=1)
        summed = jnp.einsum("pj,jf->pf", spread_weights, packed, precision=highest)
        gram_sum = summed[:, : ensemble * ensemble].reshape(count, ensemble, ensemble)
        pull_sum = summed[:, ensemble * ensemble :]
        identity = jnp.broadcast_to(
            jnp.eye(ensemble, dtype=jnp.float32), (height, ensemble, ensemble)
        )
        matrix = (ensemble - 1.0) * identity + gram_local + gram_sum
        pulled = pull_vec + pull_sum
        norm_scale = jnp.sqrt(jnp.sum(matrix * matrix, axis=(1, 2)))
        sqrt_iter = matrix / norm_scale[:, None, None]
        inverse_root = identity
        for sweep in range(NS_ITERS):
            half_step = 1.5 * identity - 0.5 * jnp.einsum(
                "pab,pbc->pac", inverse_root, sqrt_iter, precision=highest
            )
            sqrt_iter = jnp.einsum("pab,pbc->pac", sqrt_iter, half_step, precision=highest)
            inverse_root = jnp.einsum("pab,pbc->pac", half_step, inverse_root, precision=highest)
        once_applied = jnp.einsum("pab,pb->pa", inverse_root, pulled, precision=highest)
        mean_weight = (
            jnp.einsum("pab,pb->pa", inverse_root, once_applied, precision=highest)
            / norm_scale[:, None]
        )
        transform = (jnp.sqrt(ensemble - 1.0) / jnp.sqrt(norm_scale))[
            :, None, None
        ] * inverse_root + mean_weight[:, :, None]
        weights = transform + (1.0 - jnp.sum(transform, axis=1, keepdims=True)) / ensemble
        weights = jnp.take(weights, source_member, axis=1).reshape(
            height, quarters, ensemble_part, ensemble
        )
        patch_of = jnp.arange(height, dtype=jnp.int32)
        spread_out = jnp.where(
            (patch_of[:, None] == patch_of[None, :])[None, :, :, None, None, None],
            patch_block_slice.astype(jnp.float32)[:, None],
            0.0,
        )
        analysed = jnp.einsum(
            "ajnm,jailnc->mcil", weights, spread_out, precision=highest
        )
        return analysed

    return on_device


def solution(mesh):
    grp_size, band_size = mesh.devices.shape
    fine = Mesh(
        mesh.devices.reshape(grp_size // 2, 2, 2, band_size // 32 * 4, 4),
        GRP + BAND,
    )
    placed = (
        P(BAND, None, GRP, None),
        P(),
        P(),
        P(),
        P(),
        P(GRP + BAND, None),
        P(GRP + BAND, None),
        P(GRP + BAND, None),
        P(GRP + BAND, None),
        P(GRP + BAND, None),
    )
    mapped = jax.shard_map(
        make_on_device(band_size),
        mesh=fine,
        in_specs=placed,
        out_specs=P(None, None, BAND, GRP),
        check_vma=False,
    )

    def run(prior_samples, *rest):
        rows_first = with_layout_constraint(
            jnp.transpose(prior_samples, (2, 3, 0, 1)), Layout((0, 1, 2, 3))
        )
        return mapped(rows_first, *rest)

    return run
```

```python
import jax
import jax.numpy as jnp
import numpy as np
from jax import lax
from jax.experimental.layout import Layout, with_layout_constraint
from jax.sharding import Mesh
from jax.sharding import PartitionSpec as P

NS_ITERS = 6

GRP = ("y_lo", "core")
BAND = ("y_hi", "x", "z")


def shift_pairs(count, step):
    return [(i, i + step) for i in range(count) if 0 <= i + step < count]


def padded_2(cells, band_size):
    return jnp.concatenate(
        [
            lax.ppermute(cells, BAND, shift_pairs(band_size, 1)),
            cells,
            lax.ppermute(cells, BAND, shift_pairs(band_size, -1)),
        ],
        axis=0,
    )


def convolve(padded, kernel):
    wrapped = jnp.concatenate([padded[:, -1:], padded, padded[:, :1]], axis=1)
    return lax.conv_general_dilated(
        wrapped,
        kernel,
        window_strides=(1, 1),
        padding="VALID",
        dimension_numbers=("HWNC", "HWOI", "HWNC"),
        preferred_element_type=jnp.float32,
    )


def convolve_valid(padded, kernel):
    return lax.conv_general_dilated(
        padded,
        kernel,
        window_strides=(1, 1),
        padding="VALID",
        dimension_numbers=("HWNC", "HWOI", "HWNC"),
        preferred_element_type=jnp.float32,
    )


def make_on_device(band_size):
    def on_device(
        prior_samples,
        conv1_weight,
        conv1_bias,
        conv2_weight,
        conv2_bias,
        obs_index,
        obs_values,
        obs_prec,
        neighbours,
        loc_weight,
    ):
        highest = lax.Precision.HIGHEST
        rows_first = prior_samples
        height = rows_first.shape[0]
        place = lax.axis_index(BAND)
        row_ids = jnp.arange(height + 2, dtype=jnp.int32)[:, None, None, None]
        outside = ((place == 0) & (row_ids == 0)) | (
            (place == band_size - 1) & (row_ids == height + 1)
        )
        width = rows_first.shape[1]
        half = width // 2

        def forecast_of(own, padded):
            hidden_fields = jax.nn.silu(
                convolve_valid(padded, conv1_weight) + conv1_bias
            ).astype(jnp.bfloat16)
            extended = jnp.where(outside, jnp.zeros_like(hidden_fields), hidden_fields)
            return (
                own[:, 1:-1].astype(jnp.float32)
                + convolve_valid(extended, conv2_weight)
                + conv2_bias
            ).astype(jnp.bfloat16)

        send_a = jnp.concatenate([rows_first[:, width - 2 :], rows_first[:, : half + 2]], axis=1)
        send_b = jnp.concatenate([rows_first[:, half - 2 :], rows_first[:, :2]], axis=1)
        padded_a = padded_2(send_a, band_size)
        padded_a, send_b = lax.optimization_barrier((padded_a, send_b))
        padded_b = padded_2(send_b, band_size)
        forecast = jnp.concatenate(
            [
                forecast_of(send_a[:, 1:-1], padded_a),
                forecast_of(send_b[:, 1:-1], padded_b),
            ],
            axis=1,
        )
        ensemble_part = forecast.shape[2]
        channels = forecast.shape[3]
        quarters = lax.psum(1, GRP)
        patch_width = forecast.shape[1] // quarters
        blocks = forecast.reshape(height, quarters, patch_width, ensemble_part, channels)
        row_index = lax.all_gather(obs_index, GRP, axis=0, tiled=False)
        column = row_index % patch_width
        channel = row_index // patch_width
        column_hot = (
            column[..., None] == jnp.arange(patch_width, dtype=jnp.int32)
        ).astype(jnp.bfloat16)
        by_column = jnp.einsum(
            "iqlmc,qiol->qicmo",
            blocks,
            column_hot,
            preferred_element_type=jnp.float32,
        )
        channel_hot = (
            channel[:, :, None, :] == jnp.arange(channels, dtype=jnp.int32)[None, None, :, None]
        ).astype(jnp.float32)
        own_members = jnp.sum(by_column * channel_hot[:, :, :, None, :], axis=2)
        predicted = lax.all_to_all(own_members, GRP, split_axis=0, concat_axis=2, tiled=True)[0]
        me = lax.axis_index(GRP)
        pieces = [lax.dynamic_index_in_dim(blocks, me, axis=1, keepdims=False)]
        for step in range(1, quarters):
            outgoing = lax.dynamic_index_in_dim(blocks, (me + step) % quarters, axis=1, keepdims=False)
            pieces.append(
                lax.ppermute(outgoing, GRP, [(j, (j + step) % quarters) for j in range(quarters)])
            )
        patch_block_slice = jnp.stack(pieces, axis=0)
        ensemble = quarters * ensemble_part
        source_member = (
            ((me - jnp.arange(quarters, dtype=jnp.int32)) % quarters)[:, None] * ensemble_part
            + jnp.arange(ensemble_part, dtype=jnp.int32)[None, :]
        ).reshape(ensemble)
        predicted_mean = jnp.mean(predicted, axis=1)
        perturb = predicted - predicted_mean[:, None, :]
        innovation = obs_values - predicted_mean
        gram_local = jnp.einsum(
            "pmo,po,pno->pmn", perturb, obs_prec, perturb, precision=highest
        )
        pull_vec = jnp.einsum(
            "pmo,po->pm", perturb, obs_prec * innovation, precision=highest
        )
        count = gram_local.shape[0]
        packed = jnp.concatenate(
            [gram_local.reshape(count, ensemble * ensemble), pull_vec], axis=1
        )
        devices = lax.psum(1, GRP + BAND)
        packed = lax.all_to_all(
            jnp.broadcast_to(packed[None], (devices,) + packed.shape),
            GRP + BAND, split_axis=0, concat_axis=0, tiled=True,
        )
        packed = packed.reshape(-1, ensemble * ensemble + ensemble)
        total_patches = packed.shape[0]
        patch_ids = jnp.arange(total_patches, dtype=jnp.int32)
        matches = (neighbours[:, :, None] == patch_ids[None, None, :]).astype(jnp.float32)
        spread_weights = jnp.sum(loc_weight[:, :, None] * matches, axis=1)
        summed = jnp.einsum("pj,jf->pf", spread_weights, packed, precision=highest)
        gram_sum = summed[:, : ensemble * ensemble].reshape(count, ensemble, ensemble)
        pull_sum = summed[:, ensemble * ensemble :]
        identity = jnp.broadcast_to(
            jnp.eye(ensemble, dtype=jnp.float32), (height, ensemble, ensemble)
        )
        matrix = (ensemble - 1.0) * identity + gram_local + gram_sum
        pulled = pull_vec + pull_sum
        norm_scale = jnp.sqrt(jnp.sum(matrix * matrix, axis=(1, 2)))
        sqrt_iter = matrix / norm_scale[:, None, None]
        inverse_root = identity
        for sweep in range(NS_ITERS):
            half_step = 1.5 * identity - 0.5 * jnp.einsum(
                "pab,pbc->pac", inverse_root, sqrt_iter, precision=highest
            )
            sqrt_iter = jnp.einsum("pab,pbc->pac", sqrt_iter, half_step, precision=highest)
            inverse_root = jnp.einsum("pab,pbc->pac", half_step, inverse_root, precision=highest)
        once_applied = jnp.einsum("pab,pb->pa", inverse_root, pulled, precision=highest)
        mean_weight = (
            jnp.einsum("pab,pb->pa", inverse_root, once_applied, precision=highest)
            / norm_scale[:, None]
        )
        transform = (jnp.sqrt(ensemble - 1.0) / jnp.sqrt(norm_scale))[
            :, None, None
        ] * inverse_root + mean_weight[:, :, None]
        weights = transform + (1.0 - jnp.sum(transform, axis=1, keepdims=True)) / ensemble
        weights = jnp.take(weights, source_member, axis=1).reshape(
            height, quarters, ensemble_part, ensemble
        )
        patch_of = jnp.arange(height, dtype=jnp.int32)
        spread_out = jnp.where(
            (patch_of[:, None] == patch_of[None, :])[None, :, :, None, None, None],
            patch_block_slice.astype(jnp.float32)[:, None],
            0.0,
        )
        analysed = jnp.einsum(
            "ajnm,jailnc->mcil", weights, spread_out, precision=highest
        )
        return analysed

    return on_device


def solution(mesh):
    grp_size, band_size = mesh.devices.shape
    fine = Mesh(
        mesh.devices.reshape(grp_size // 2, 2, 2, band_size // 32 * 4, 4),
        GRP + BAND,
    )
    placed = (
        P(BAND, None, GRP, None),
        P(),
        P(),
        P(),
        P(),
        P(GRP + BAND, None),
        P(GRP + BAND, None),
        P(GRP + BAND, None),
        P(GRP + BAND, None),
        P(GRP + BAND, None),
    )
    mapped = jax.shard_map(
        make_on_device(band_size),
        mesh=fine,
        in_specs=placed,
        out_specs=P(None, None, BAND, GRP),
        check_vma=False,
    )

    def run(prior_samples, *rest):
        rows_first = with_layout_constraint(
            jnp.transpose(prior_samples, (2, 3, 0, 1)), Layout((0, 1, 2, 3))
        )
        return mapped(rows_first, *rest)

    return run
```

```python
import jax
import jax.numpy as jnp
import numpy as np
from jax import lax
from jax.experimental.layout import Layout, with_layout_constraint
from jax.sharding import Mesh
from jax.sharding import PartitionSpec as P

NS_ITERS = 6

GRP = ("y_lo", "core")
BAND = ("y_hi", "x", "z")


def shift_pairs(count, step):
    return [(i, i + step) for i in range(count) if 0 <= i + step < count]


def padded_2(cells, band_size):
    return jnp.concatenate(
        [
            lax.ppermute(cells, BAND, shift_pairs(band_size, 1)),
            cells,
            lax.ppermute(cells, BAND, shift_pairs(band_size, -1)),
        ],
        axis=0,
    )


def convolve(padded, kernel):
    wrapped = jnp.concatenate([padded[:, -1:], padded, padded[:, :1]], axis=1)
    return lax.conv_general_dilated(
        wrapped,
        kernel,
        window_strides=(1, 1),
        padding="VALID",
        dimension_numbers=("HWNC", "HWOI", "HWNC"),
        preferred_element_type=jnp.float32,
    )


def make_on_device(band_size):
    def on_device(
        prior_samples,
        conv1_weight,
        conv1_bias,
        conv2_weight,
        conv2_bias,
        obs_index,
        obs_values,
        obs_prec,
        neighbours,
        loc_weight,
    ):
        highest = lax.Precision.HIGHEST
        rows_first = prior_samples
        height = rows_first.shape[0]
        padded = padded_2(rows_first, band_size)
        hidden_fields = jax.nn.silu(
            convolve(padded, conv1_weight) + conv1_bias
        ).astype(jnp.bfloat16)
        place = lax.axis_index(BAND)
        row_ids = jnp.arange(height + 2, dtype=jnp.int32)[:, None, None, None]
        outside = ((place == 0) & (row_ids == 0)) | (
            (place == band_size - 1) & (row_ids == height + 1)
        )
        extended = jnp.where(outside, jnp.zeros_like(hidden_fields), hidden_fields)
        forecast = (
            rows_first.astype(jnp.float32)
            + convolve(extended, conv2_weight)
            + conv2_bias
        ).astype(jnp.bfloat16)
        ensemble_part = forecast.shape[2]
        channels = forecast.shape[3]
        quarters = lax.psum(1, GRP)
        patch_width = forecast.shape[1] // quarters
        blocks = forecast.reshape(height, quarters, patch_width, ensemble_part, channels)
        row_index = lax.all_gather(obs_index, GRP, axis=0, tiled=False)
        column = row_index % patch_width
        channel = row_index // patch_width
        column_hot = (
            column[..., None] == jnp.arange(patch_width, dtype=jnp.int32)
        ).astype(jnp.bfloat16)
        by_column = jnp.einsum(
            "iqlmc,qiol->qicmo",
            blocks,
            column_hot,
            preferred_element_type=jnp.float32,
        )
        channel_hot = (
            channel[:, :, None, :] == jnp.arange(channels, dtype=jnp.int32)[None, None, :, None]
        ).astype(jnp.float32)
        own_members = jnp.sum(by_column * channel_hot[:, :, :, None, :], axis=2)
        predicted = lax.all_to_all(own_members, GRP, split_axis=0, concat_axis=2, tiled=True)[0]
        me = lax.axis_index(GRP)
        pieces = [lax.dynamic_index_in_dim(blocks, me, axis=1, keepdims=False)]
        for step in range(1, quarters):
            outgoing = lax.dynamic_index_in_dim(blocks, (me + step) % quarters, axis=1, keepdims=False)
            pieces.append(
                lax.ppermute(outgoing, GRP, [(j, (j + step) % quarters) for j in range(quarters)])
            )
        patch_block_slice = jnp.stack(pieces, axis=0)
        ensemble = quarters * ensemble_part
        source_member = (
            ((me - jnp.arange(quarters, dtype=jnp.int32)) % quarters)[:, None] * ensemble_part
            + jnp.arange(ensemble_part, dtype=jnp.int32)[None, :]
        ).reshape(ensemble)
        predicted_mean = jnp.mean(predicted, axis=1)
        perturb = predicted - predicted_mean[:, None, :]
        innovation = obs_values - predicted_mean
        gram_local = jnp.einsum(
            "pmo,po,pno->pmn", perturb, obs_prec, perturb, precision=highest
        )
        pull_vec = jnp.einsum(
            "pmo,po->pm", perturb, obs_prec * innovation, precision=highest
        )
        count = gram_local.shape[0]
        upper_rows, upper_cols = np.triu_indices(ensemble)
        upper = upper_rows * ensemble + upper_cols
        triangle = upper.shape[0]
        place_of = np.zeros((ensemble, ensemble), np.int32)
        place_of[upper_rows, upper_cols] = np.arange(triangle)
        place_of[upper_cols, upper_rows] = np.arange(triangle)
        packed = jnp.concatenate(
            [gram_local.reshape(count, ensemble * ensemble)[:, upper], pull_vec], axis=1
        )
        devices = lax.psum(1, GRP + BAND)
        packed = lax.all_to_all(
            jnp.broadcast_to(packed[None], (devices,) + packed.shape),
            GRP + BAND, split_axis=0, concat_axis=0, tiled=True,
        )
        packed = packed.reshape(-1, triangle + ensemble)
        total_patches = packed.shape[0]
        patch_ids = jnp.arange(total_patches, dtype=jnp.int32)
        matches = (neighbours[:, :, None] == patch_ids[None, None, :]).astype(jnp.float32)
        spread_weights = jnp.sum(loc_weight[:, :, None] * matches, axis=1)
        summed = jnp.einsum("pj,jf->pf", spread_weights, packed, precision=highest)
        gram_sum = summed[:, place_of.reshape(-1)].reshape(count, ensemble, ensemble)
        pull_sum = summed[:, triangle:]
        identity = jnp.broadcast_to(
            jnp.eye(ensemble, dtype=jnp.float32), (height, ensemble, ensemble)
        )
        matrix = (ensemble - 1.0) * identity + gram_local + gram_sum
        pulled = pull_vec + pull_sum
        norm_scale = jnp.sqrt(jnp.sum(matrix * matrix, axis=(1, 2)))
        sqrt_iter = matrix / norm_scale[:, None, None]
        inverse_root = identity
        for sweep in range(NS_ITERS):
            half_step = 1.5 * identity - 0.5 * jnp.einsum(
                "pab,pbc->pac", inverse_root, sqrt_iter, precision=highest
            )
            sqrt_iter = jnp.einsum("pab,pbc->pac", sqrt_iter, half_step, precision=highest)
            inverse_root = jnp.einsum("pab,pbc->pac", half_step, inverse_root, precision=highest)
        once_applied = jnp.einsum("pab,pb->pa", inverse_root, pulled, precision=highest)
        mean_weight = (
            jnp.einsum("pab,pb->pa", inverse_root, once_applied, precision=highest)
            / norm_scale[:, None]
        )
        transform = (jnp.sqrt(ensemble - 1.0) / jnp.sqrt(norm_scale))[
            :, None, None
        ] * inverse_root + mean_weight[:, :, None]
        weights = transform + (1.0 - jnp.sum(transform, axis=1, keepdims=True)) / ensemble
        weights = jnp.take(weights, source_member, axis=1).reshape(
            height, quarters, ensemble_part, ensemble
        )
        patch_of = jnp.arange(height, dtype=jnp.int32)
        spread_out = jnp.where(
            (patch_of[:, None] == patch_of[None, :])[None, :, :, None, None, None],
            patch_block_slice.astype(jnp.float32)[:, None],
            0.0,
        )
        analysed = jnp.einsum(
            "ajnm,jailnc->mcil", weights, spread_out, precision=highest
        )
        return analysed

    return on_device


def solution(mesh):
    grp_size, band_size = mesh.devices.shape
    fine = Mesh(
        mesh.devices.reshape(grp_size // 2, 2, 2, band_size // 32 * 4, 4),
        GRP + BAND,
    )
    placed = (
        P(BAND, None, GRP, None),
        P(),
        P(),
        P(),
        P(),
        P(GRP + BAND, None),
        P(GRP + BAND, None),
        P(GRP + BAND, None),
        P(GRP + BAND, None),
        P(GRP + BAND, None),
    )
    mapped = jax.shard_map(
        make_on_device(band_size),
        mesh=fine,
        in_specs=placed,
        out_specs=P(None, None, BAND, GRP),
        check_vma=False,
    )

    def run(prior_samples, *rest):
        rows_first = with_layout_constraint(
            jnp.transpose(prior_samples, (2, 3, 0, 1)), Layout((0, 1, 2, 3))
        )
        return mapped(rows_first, *rest)

    return run
```

```python
import jax
import jax.numpy as jnp
import numpy as np
from jax import lax
from jax.experimental.layout import Layout, with_layout_constraint
from jax.sharding import Mesh
from jax.sharding import PartitionSpec as P

NS_ITERS = 6

GRP = ("y_lo", "core")
BAND = ("y_hi", "x", "z")


def shift_pairs(count, step):
    return [(i, i + step) for i in range(count) if 0 <= i + step < count]


def padded_2(cells, band_size):
    return jnp.concatenate(
        [
            lax.ppermute(cells, BAND, shift_pairs(band_size, 1)),
            cells,
            lax.ppermute(cells, BAND, shift_pairs(band_size, -1)),
        ],
        axis=0,
    )


def convolve(padded, kernel):
    wrapped = jnp.concatenate([padded[:, -1:], padded, padded[:, :1]], axis=1)
    return lax.conv_general_dilated(
        wrapped,
        kernel,
        window_strides=(1, 1),
        padding="VALID",
        dimension_numbers=("HWNC", "HWOI", "HWNC"),
        preferred_element_type=jnp.float32,
    )


def make_on_device(band_size):
    def on_device(
        prior_samples,
        conv1_weight,
        conv1_bias,
        conv2_weight,
        conv2_bias,
        obs_index,
        obs_values,
        obs_prec,
        neighbours,
        loc_weight,
    ):
        highest = lax.Precision.HIGHEST
        rows_first = prior_samples
        height = rows_first.shape[0]
        padded = padded_2(rows_first, band_size)
        hidden_fields = jax.nn.silu(
            convolve(padded, conv1_weight) + conv1_bias
        ).astype(jnp.bfloat16)
        place = lax.axis_index(BAND)
        row_ids = jnp.arange(height + 2, dtype=jnp.int32)[:, None, None, None]
        outside = ((place == 0) & (row_ids == 0)) | (
            (place == band_size - 1) & (row_ids == height + 1)
        )
        extended = jnp.where(outside, jnp.zeros_like(hidden_fields), hidden_fields)
        forecast = (
            rows_first.astype(jnp.float32)
            + convolve(extended, conv2_weight)
            + conv2_bias
        ).astype(jnp.bfloat16)
        ensemble_part = forecast.shape[2]
        channels = forecast.shape[3]
        quarters = lax.psum(1, GRP)
        patch_width = forecast.shape[1] // quarters
        blocks = forecast.reshape(height, quarters, patch_width, ensemble_part, channels)
        me = lax.axis_index(GRP)
        outgoing = [
            lax.dynamic_index_in_dim(blocks, (me + step) % quarters, axis=1, keepdims=False)
            for step in range(quarters)
        ]
        outgoing, blocks = lax.optimization_barrier((outgoing, blocks))
        pieces = [outgoing[0]] + [
            lax.ppermute(outgoing[step], GRP, [(j, (j + step) % quarters) for j in range(quarters)])
            for step in range(1, quarters)
        ]
        patch_block_slice = jnp.stack(pieces, axis=0)
        row_index = lax.all_gather(obs_index, GRP, axis=0, tiled=False)
        column = row_index % patch_width
        channel = row_index // patch_width
        column_hot = (
            column[..., None] == jnp.arange(patch_width, dtype=jnp.int32)
        ).astype(jnp.bfloat16)
        by_column = jnp.einsum(
            "iqlmc,qiol->qicmo",
            blocks,
            column_hot,
            preferred_element_type=jnp.float32,
        )
        channel_hot = (
            channel[:, :, None, :] == jnp.arange(channels, dtype=jnp.int32)[None, None, :, None]
        ).astype(jnp.float32)
        own_members = jnp.sum(by_column * channel_hot[:, :, :, None, :], axis=2)
        got = [lax.dynamic_index_in_dim(own_members, me, axis=0, keepdims=False)] + [
            lax.ppermute(
                lax.dynamic_index_in_dim(own_members, (me + step) % quarters, axis=0, keepdims=False),
                GRP,
                [(j, (j + step) % quarters) for j in range(quarters)],
            )
            for step in range(1, quarters)
        ]
        member_ids = jnp.arange(quarters * ensemble_part, dtype=jnp.int32)
        in_order = (
            (me - member_ids // ensemble_part) % quarters * ensemble_part
            + member_ids % ensemble_part
        )
        predicted = jnp.take(jnp.concatenate(got, axis=1), in_order, axis=1)
        ensemble = quarters * ensemble_part
        source_member = (
            ((me - jnp.arange(quarters, dtype=jnp.int32)) % quarters)[:, None] * ensemble_part
            + jnp.arange(ensemble_part, dtype=jnp.int32)[None, :]
        ).reshape(ensemble)
        predicted_mean = jnp.mean(predicted, axis=1)
        perturb = predicted - predicted_mean[:, None, :]
        innovation = obs_values - predicted_mean
        gram_local = jnp.einsum(
            "pmo,po,pno->pmn", perturb, obs_prec, perturb, precision=highest
        )
        pull_vec = jnp.einsum(
            "pmo,po->pm", perturb, obs_prec * innovation, precision=highest
        )
        count = gram_local.shape[0]
        upper_rows, upper_cols = np.triu_indices(ensemble)
        upper = upper_rows * ensemble + upper_cols
        triangle = upper.shape[0]
        place_of = np.zeros((ensemble, ensemble), np.int32)
        place_of[upper_rows, upper_cols] = np.arange(triangle)
        place_of[upper_cols, upper_rows] = np.arange(triangle)
        packed = jnp.concatenate(
            [gram_local.reshape(count, ensemble * ensemble)[:, upper], pull_vec], axis=1
        )
        devices = lax.psum(1, GRP + BAND)
        packed = lax.all_to_all(
            jnp.broadcast_to(packed[None], (devices,) + packed.shape),
            GRP + BAND, split_axis=0, concat_axis=0, tiled=True,
        )
        packed = packed.reshape(-1, triangle + ensemble)
        total_patches = packed.shape[0]
        patch_ids = jnp.arange(total_patches, dtype=jnp.int32)
        matches = (neighbours[:, :, None] == patch_ids[None, None, :]).astype(jnp.float32)
        spread_weights = jnp.sum(loc_weight[:, :, None] * matches, axis=1)
        summed = jnp.einsum("pj,jf->pf", spread_weights, packed, precision=highest)
        gram_sum = summed[:, place_of.reshape(-1)].reshape(count, ensemble, ensemble)
        pull_sum = summed[:, triangle:]
        identity = jnp.broadcast_to(
            jnp.eye(ensemble, dtype=jnp.float32), (height, ensemble, ensemble)
        )
        matrix = (ensemble - 1.0) * identity + gram_local + gram_sum
        pulled = pull_vec + pull_sum
        norm_scale = jnp.sqrt(jnp.sum(matrix * matrix, axis=(1, 2)))
        sqrt_iter = matrix / norm_scale[:, None, None]
        inverse_root = identity
        for sweep in range(NS_ITERS):
            half_step = 1.5 * identity - 0.5 * jnp.einsum(
                "pab,pbc->pac", inverse_root, sqrt_iter, precision=highest
            )
            sqrt_iter = jnp.einsum("pab,pbc->pac", sqrt_iter, half_step, precision=highest)
            inverse_root = jnp.einsum("pab,pbc->pac", half_step, inverse_root, precision=highest)
        once_applied = jnp.einsum("pab,pb->pa", inverse_root, pulled, precision=highest)
        mean_weight = (
            jnp.einsum("pab,pb->pa", inverse_root, once_applied, precision=highest)
            / norm_scale[:, None]
        )
        transform = (jnp.sqrt(ensemble - 1.0) / jnp.sqrt(norm_scale))[
            :, None, None
        ] * inverse_root + mean_weight[:, :, None]
        weights = transform + (1.0 - jnp.sum(transform, axis=1, keepdims=True)) / ensemble
        weights = jnp.take(weights, source_member, axis=1).reshape(
            height, quarters, ensemble_part, ensemble
        )
        patch_of = jnp.arange(height, dtype=jnp.int32)
        spread_out = jnp.where(
            (patch_of[:, None] == patch_of[None, :])[None, :, :, None, None, None],
            patch_block_slice.astype(jnp.float32)[:, None],
            0.0,
        )
        analysed = jnp.einsum(
            "ajnm,jailnc->mcil", weights, spread_out, precision=highest
        )
        return analysed

    return on_device


def solution(mesh):
    grp_size, band_size = mesh.devices.shape
    fine = Mesh(
        mesh.devices.reshape(grp_size // 2, 2, 2, band_size // 32 * 4, 4),
        GRP + BAND,
    )
    placed = (
        P(BAND, None, GRP, None),
        P(),
        P(),
        P(),
        P(),
        P(GRP + BAND, None),
        P(GRP + BAND, None),
        P(GRP + BAND, None),
        P(GRP + BAND, None),
        P(GRP + BAND, None),
    )
    mapped = jax.shard_map(
        make_on_device(band_size),
        mesh=fine,
        in_specs=placed,
        out_specs=P(None, None, BAND, GRP),
        check_vma=False,
    )

    def run(prior_samples, *rest):
        rows_first = with_layout_constraint(
            jnp.transpose(prior_samples, (2, 3, 0, 1)), Layout((0, 1, 2, 3))
        )
        return mapped(rows_first, *rest)

    return run
```

```python
import jax
import jax.numpy as jnp
import numpy as np
from jax import lax
from jax.experimental.layout import Layout, with_layout_constraint
from jax.sharding import Mesh
from jax.sharding import PartitionSpec as P

NS_ITERS = 6

GRP = ("y_lo", "core")
BAND = ("y_hi", "x", "z")


def shift_pairs(count, step):
    return [(i, i + step) for i in range(count) if 0 <= i + step < count]


def padded_2(cells, band_size):
    return jnp.concatenate(
        [
            lax.ppermute(cells, BAND, shift_pairs(band_size, 1)),
            cells,
            lax.ppermute(cells, BAND, shift_pairs(band_size, -1)),
        ],
        axis=0,
    )


def convolve(padded, kernel):
    wrapped = jnp.concatenate([padded[:, -1:], padded, padded[:, :1]], axis=1)
    return lax.conv_general_dilated(
        wrapped,
        kernel,
        window_strides=(1, 1),
        padding="VALID",
        dimension_numbers=("HWNC", "HWOI", "HWNC"),
        preferred_element_type=jnp.float32,
    )


def make_on_device(band_size):
    def on_device(
        prior_samples,
        conv1_weight,
        conv1_bias,
        conv2_weight,
        conv2_bias,
        obs_index,
        obs_values,
        obs_prec,
        neighbours,
        loc_weight,
    ):
        highest = lax.Precision.HIGHEST
        rows_first = prior_samples
        height = rows_first.shape[0]
        padded = padded_2(rows_first, band_size)
        hidden_fields = jax.nn.silu(
            convolve(padded, conv1_weight) + conv1_bias
        ).astype(jnp.bfloat16)
        place = lax.axis_index(BAND)
        row_ids = jnp.arange(height + 2, dtype=jnp.int32)[:, None, None, None]
        outside = ((place == 0) & (row_ids == 0)) | (
            (place == band_size - 1) & (row_ids == height + 1)
        )
        extended = jnp.where(outside, jnp.zeros_like(hidden_fields), hidden_fields)
        forecast = (
            rows_first.astype(jnp.float32)
            + convolve(extended, conv2_weight)
            + conv2_bias
        ).astype(jnp.bfloat16)
        ensemble_part = forecast.shape[2]
        channels = forecast.shape[3]
        quarters = lax.psum(1, GRP)
        patch_width = forecast.shape[1] // quarters
        blocks = forecast.reshape(height, quarters, patch_width, ensemble_part, channels)
        row_index = lax.all_gather(obs_index, GRP, axis=0, tiled=False)
        column = row_index % patch_width
        channel = row_index // patch_width
        column_hot = (
            column[..., None] == jnp.arange(patch_width, dtype=jnp.int32)
        ).astype(jnp.bfloat16)
        by_column = jnp.einsum(
            "iqlmc,qiol->qicmo",
            blocks,
            column_hot,
            preferred_element_type=jnp.float32,
        )
        channel_hot = (
            channel[:, :, None, :] == jnp.arange(channels, dtype=jnp.int32)[None, None, :, None]
        ).astype(jnp.float32)
        own_members = jnp.sum(by_column * channel_hot[:, :, :, None, :], axis=2)
        predicted = lax.all_to_all(own_members, GRP, split_axis=0, concat_axis=2, tiled=True)[0]
        me = lax.axis_index(GRP)
        pieces = [lax.dynamic_index_in_dim(blocks, me, axis=1, keepdims=False)]
        for step in range(1, quarters):
            outgoing = lax.dynamic_index_in_dim(blocks, (me + step) % quarters, axis=1, keepdims=False)
            pieces.append(
                lax.ppermute(outgoing, GRP, [(j, (j + step) % quarters) for j in range(quarters)])
            )
        patch_block_slice = jnp.stack(pieces, axis=0)
        ensemble = quarters * ensemble_part
        source_member = (
            ((me - jnp.arange(quarters, dtype=jnp.int32)) % quarters)[:, None] * ensemble_part
            + jnp.arange(ensemble_part, dtype=jnp.int32)[None, :]
        ).reshape(ensemble)
        predicted_mean = jnp.mean(predicted, axis=1)
        perturb = predicted - predicted_mean[:, None, :]
        innovation = obs_values - predicted_mean
        gram_local = jnp.einsum(
            "pmo,po,pno->pmn", perturb, obs_prec, perturb, precision=highest
        )
        pull_vec = jnp.einsum(
            "pmo,po->pm", perturb, obs_prec * innovation, precision=highest
        )
        count = gram_local.shape[0]
        upper_rows, upper_cols = np.triu_indices(ensemble)
        upper = upper_rows * ensemble + upper_cols
        triangle = upper.shape[0]
        place_of = np.zeros((ensemble, ensemble), np.int32)
        place_of[upper_rows, upper_cols] = np.arange(triangle)
        place_of[upper_cols, upper_rows] = np.arange(triangle)
        packed = jnp.concatenate(
            [gram_local.reshape(count, ensemble * ensemble)[:, upper], pull_vec], axis=1
        )
        devices = lax.psum(1, GRP + BAND)
        packed = lax.all_to_all(
            jnp.broadcast_to(packed[None], (devices,) + packed.shape),
            GRP + BAND, split_axis=0, concat_axis=0, tiled=True,
        )
        packed = packed.reshape(-1, triangle + ensemble)
        total_patches = packed.shape[0]
        patch_ids = jnp.arange(total_patches, dtype=jnp.int32)
        matches = (neighbours[:, :, None] == patch_ids[None, None, :]).astype(jnp.float32)
        spread_weights = jnp.sum(loc_weight[:, :, None] * matches, axis=1)
        summed = jnp.einsum("pj,jf->pf", spread_weights, packed, precision=highest)
        gram_sum = summed[:, place_of.reshape(-1)].reshape(count, ensemble, ensemble)
        pull_sum = summed[:, triangle:]
        identity = jnp.broadcast_to(
            jnp.eye(ensemble, dtype=jnp.float32), (height, ensemble, ensemble)
        )
        matrix = (ensemble - 1.0) * identity + gram_local + gram_sum
        pulled = pull_vec + pull_sum
        norm_scale = jnp.sqrt(jnp.sum(matrix * matrix, axis=(1, 2)))
        sqrt_iter = matrix / norm_scale[:, None, None]
        inverse_root = identity
        for sweep in range(NS_ITERS):
            half_step = 1.5 * identity - 0.5 * jnp.einsum(
                "pab,pbc->pac", inverse_root, sqrt_iter, precision=highest
            )
            both = jnp.einsum(
                "pab,pbc->pac",
                half_step,
                jnp.concatenate([sqrt_iter, inverse_root], axis=2),
                precision=highest,
            )
            sqrt_iter = both[:, :, :ensemble]
            inverse_root = both[:, :, ensemble:]
        once_applied = jnp.einsum("pab,pb->pa", inverse_root, pulled, precision=highest)
        mean_weight = (
            jnp.einsum("pab,pb->pa", inverse_root, once_applied, precision=highest)
            / norm_scale[:, None]
        )
        transform = (jnp.sqrt(ensemble - 1.0) / jnp.sqrt(norm_scale))[
            :, None, None
        ] * inverse_root + mean_weight[:, :, None]
        weights = transform + (1.0 - jnp.sum(transform, axis=1, keepdims=True)) / ensemble
        weights = jnp.take(weights, source_member, axis=1).reshape(
            height, quarters, ensemble_part, ensemble
        )
        patch_of = jnp.arange(height, dtype=jnp.int32)
        spread_out = jnp.where(
            (patch_of[:, None] == patch_of[None, :])[None, :, :, None, None, None],
            patch_block_slice.astype(jnp.float32)[:, None],
            0.0,
        )
        analysed = jnp.einsum(
            "ajnm,jailnc->mcil", weights, spread_out, precision=highest
        )
        return analysed

    return on_device


def solution(mesh):
    grp_size, band_size = mesh.devices.shape
    fine = Mesh(
        mesh.devices.reshape(grp_size // 2, 2, 2, band_size // 32 * 4, 4),
        GRP + BAND,
    )
    placed = (
        P(BAND, None, GRP, None),
        P(),
        P(),
        P(),
        P(),
        P(GRP + BAND, None),
        P(GRP + BAND, None),
        P(GRP + BAND, None),
        P(GRP + BAND, None),
        P(GRP + BAND, None),
    )
    mapped = jax.shard_map(
        make_on_device(band_size),
        mesh=fine,
        in_specs=placed,
        out_specs=P(None, None, BAND, GRP),
        check_vma=False,
    )

    def run(prior_samples, *rest):
        rows_first = with_layout_constraint(
            jnp.transpose(prior_samples, (2, 3, 0, 1)), Layout((0, 1, 2, 3))
        )
        return mapped(rows_first, *rest)

    return run
```

```python
import jax
import jax.numpy as jnp
import numpy as np
from jax import lax
from jax.experimental.layout import Layout, with_layout_constraint
from jax.sharding import Mesh
from jax.sharding import PartitionSpec as P

NS_ITERS = 6

GRP = ("y_lo", "core")
BAND = ("y_hi", "x", "z")


def shift_pairs(count, step):
    return [(i, i + step) for i in range(count) if 0 <= i + step < count]


def padded_2(cells, band_size):
    return jnp.concatenate(
        [
            lax.ppermute(cells, BAND, shift_pairs(band_size, 1)),
            cells,
            lax.ppermute(cells, BAND, shift_pairs(band_size, -1)),
        ],
        axis=0,
    )


def convolve(padded, kernel):
    wrapped = jnp.concatenate([padded[:, -1:], padded, padded[:, :1]], axis=1)
    return lax.conv_general_dilated(
        wrapped,
        kernel,
        window_strides=(1, 1),
        padding="VALID",
        dimension_numbers=("HWNC", "HWOI", "HWNC"),
        preferred_element_type=jnp.float32,
    )


def make_on_device(band_size):
    def on_device(
        prior_samples,
        conv1_weight,
        conv1_bias,
        conv2_weight,
        conv2_bias,
        obs_index,
        obs_values,
        obs_prec,
        neighbours,
        loc_weight,
    ):
        highest = lax.Precision.HIGHEST
        rows_first = prior_samples
        height = rows_first.shape[0]
        padded = padded_2(rows_first, band_size)
        hidden_fields = jax.nn.silu(
            convolve(padded, conv1_weight) + conv1_bias
        ).astype(jnp.bfloat16)
        place = lax.axis_index(BAND)
        row_ids = jnp.arange(height + 2, dtype=jnp.int32)[:, None, None, None]
        outside = ((place == 0) & (row_ids == 0)) | (
            (place == band_size - 1) & (row_ids == height + 1)
        )
        extended = jnp.where(outside, jnp.zeros_like(hidden_fields), hidden_fields)
        forecast = (
            rows_first.astype(jnp.float32)
            + convolve(extended, conv2_weight)
            + conv2_bias
        ).astype(jnp.bfloat16)
        ensemble_part = forecast.shape[2]
        channels = forecast.shape[3]
        quarters = lax.psum(1, GRP)
        patch_width = forecast.shape[1] // quarters
        blocks = forecast.reshape(height, quarters, patch_width, ensemble_part, channels)
        row_index = lax.all_gather(obs_index, GRP, axis=0, tiled=False)
        column = row_index % patch_width
        channel = row_index // patch_width
        column_hot = (
            column[..., None] == jnp.arange(patch_width, dtype=jnp.int32)
        ).astype(jnp.bfloat16)
        by_column = jnp.einsum(
            "iqlmc,qiol->qicmo",
            blocks,
            column_hot,
            preferred_element_type=jnp.float32,
        )
        channel_hot = (
            channel[:, :, None, :] == jnp.arange(channels, dtype=jnp.int32)[None, None, :, None]
        ).astype(jnp.float32)
        own_members = jnp.sum(by_column * channel_hot[:, :, :, None, :], axis=2)
        predicted = lax.all_to_all(own_members, GRP, split_axis=0, concat_axis=2, tiled=True)[0]
        me = lax.axis_index(GRP)
        pieces = [lax.dynamic_index_in_dim(blocks, me, axis=1, keepdims=False)]
        for step in range(1, quarters):
            outgoing = lax.dynamic_index_in_dim(blocks, (me + step) % quarters, axis=1, keepdims=False)
            pieces.append(
                lax.ppermute(outgoing, GRP, [(j, (j + step) % quarters) for j in range(quarters)])
            )
        patch_block_slice = jnp.stack(pieces, axis=0)
        ensemble = quarters * ensemble_part
        source_member = (
            ((me - jnp.arange(quarters, dtype=jnp.int32)) % quarters)[:, None] * ensemble_part
            + jnp.arange(ensemble_part, dtype=jnp.int32)[None, :]
        ).reshape(ensemble)
        predicted_mean = jnp.mean(predicted, axis=1)
        perturb = predicted - predicted_mean[:, None, :]
        innovation = obs_values - predicted_mean
        gram_local = jnp.einsum(
            "pmo,po,pno->pmn", perturb, obs_prec, perturb, precision=highest
        )
        pull_vec = jnp.einsum(
            "pmo,po->pm", perturb, obs_prec * innovation, precision=highest
        )
        count = gram_local.shape[0]
        upper_rows, upper_cols = np.triu_indices(ensemble)
        upper = upper_rows * ensemble + upper_cols
        triangle = upper.shape[0]
        place_of = np.zeros((ensemble, ensemble), np.int32)
        place_of[upper_rows, upper_cols] = np.arange(triangle)
        place_of[upper_cols, upper_rows] = np.arange(triangle)
        packed = jnp.concatenate(
            [gram_local.reshape(count, ensemble * ensemble)[:, upper], pull_vec], axis=1
        )
        devices = lax.psum(1, GRP + BAND)
        packed = lax.all_to_all(
            jnp.broadcast_to(packed[None], (devices,) + packed.shape),
            GRP + BAND, split_axis=0, concat_axis=0, tiled=True,
        )
        packed = packed.reshape(-1, triangle + ensemble)
        total_patches = packed.shape[0]
        patch_ids = jnp.arange(total_patches, dtype=jnp.int32)
        matches = (neighbours[:, :, None] == patch_ids[None, None, :]).astype(jnp.float32)
        spread_weights = jnp.sum(loc_weight[:, :, None] * matches, axis=1)
        summed = jnp.einsum("pj,jf->pf", spread_weights, packed, precision=highest)
        gram_sum = summed[:, place_of.reshape(-1)].reshape(count, ensemble, ensemble)
        pull_sum = summed[:, triangle:]
        identity = jnp.broadcast_to(
            jnp.eye(ensemble, dtype=jnp.float32), (height, ensemble, ensemble)
        )
        matrix = (ensemble - 1.0) * identity + gram_local + gram_sum
        pulled = pull_vec + pull_sum
        norm_scale = jnp.sqrt(jnp.sum(matrix * matrix, axis=(1, 2)))
        sqrt_iter = matrix / norm_scale[:, None, None]
        inverse_root = identity
        for sweep in range(NS_ITERS):
            half_step = 1.5 * identity - 0.5 * jnp.einsum(
                "pab,pbc->pac", inverse_root, sqrt_iter, precision=highest
            )
            sqrt_iter = jnp.einsum("pab,pbc->pac", sqrt_iter, half_step, precision=highest)
            inverse_root = jnp.einsum("pab,pbc->pac", half_step, inverse_root, precision=highest)
        once_applied = jnp.einsum("pab,pb->pa", inverse_root, pulled, precision=highest)
        mean_weight = (
            jnp.einsum("pab,pb->pa", inverse_root, once_applied, precision=highest)
            / norm_scale[:, None]
        )
        transform = (jnp.sqrt(ensemble - 1.0) / jnp.sqrt(norm_scale))[
            :, None, None
        ] * inverse_root + mean_weight[:, :, None]
        weights = transform + (1.0 - jnp.sum(transform, axis=1, keepdims=True)) / ensemble
        weights = jnp.take(weights, source_member, axis=1).reshape(
            height, quarters, ensemble_part, ensemble
        )
        analysed = jnp.stack(
            [
                jnp.einsum(
                    "jnm,jlnc->mcl",
                    weights[row],
                    patch_block_slice[:, row].astype(jnp.float32),
                    precision=highest,
                )
                for row in range(height)
            ],
            axis=2,
        )
        return analysed

    return on_device


def solution(mesh):
    grp_size, band_size = mesh.devices.shape
    fine = Mesh(
        mesh.devices.reshape(grp_size // 2, 2, 2, band_size // 32 * 4, 4),
        GRP + BAND,
    )
    placed = (
        P(BAND, None, GRP, None),
        P(),
        P(),
        P(),
        P(),
        P(GRP + BAND, None),
        P(GRP + BAND, None),
        P(GRP + BAND, None),
        P(GRP + BAND, None),
        P(GRP + BAND, None),
    )
    mapped = jax.shard_map(
        make_on_device(band_size),
        mesh=fine,
        in_specs=placed,
        out_specs=P(None, None, BAND, GRP),
        check_vma=False,
    )

    def run(prior_samples, *rest):
        rows_first = with_layout_constraint(
            jnp.transpose(prior_samples, (2, 3, 0, 1)), Layout((0, 1, 2, 3))
        )
        return mapped(rows_first, *rest)

    return run
```

```python
import jax
import jax.numpy as jnp
import numpy as np
from jax import lax
from jax.experimental.layout import Layout, with_layout_constraint
from jax.sharding import Mesh
from jax.sharding import PartitionSpec as P

NS_ITERS = 6

GRP = ("y_lo", "core")
BAND = ("y_hi", "x", "z")


def shift_pairs(count, step):
    return [(i, i + step) for i in range(count) if 0 <= i + step < count]


def padded_2(cells, band_size):
    return jnp.concatenate(
        [
            lax.ppermute(cells, BAND, shift_pairs(band_size, 1)),
            cells,
            lax.ppermute(cells, BAND, shift_pairs(band_size, -1)),
        ],
        axis=0,
    )


def convolve(padded, kernel):
    wrapped = jnp.concatenate([padded[:, -1:], padded, padded[:, :1]], axis=1)
    return lax.conv_general_dilated(
        wrapped,
        kernel,
        window_strides=(1, 1),
        padding="VALID",
        dimension_numbers=("HWNC", "HWOI", "HWNC"),
        preferred_element_type=jnp.float32,
    )


def make_on_device(band_size):
    def on_device(
        prior_samples,
        conv1_weight,
        conv1_bias,
        conv2_weight,
        conv2_bias,
        obs_index,
        obs_values,
        obs_prec,
        neighbours,
        loc_weight,
    ):
        highest = lax.Precision.HIGHEST
        rows_first = prior_samples
        height = rows_first.shape[0]
        padded = padded_2(rows_first, band_size)
        channels_in = padded.shape[3]
        hidden_fields = jax.nn.silu(
            convolve(
                jnp.pad(padded, ((0, 0), (0, 0), (0, 0), (0, 128 - channels_in))),
                jnp.pad(conv1_weight, ((0, 0), (0, 0), (0, 0), (0, 128 - channels_in))),
            )
            + conv1_bias
        ).astype(jnp.bfloat16)
        place = lax.axis_index(BAND)
        row_ids = jnp.arange(height + 2, dtype=jnp.int32)[:, None, None, None]
        outside = ((place == 0) & (row_ids == 0)) | (
            (place == band_size - 1) & (row_ids == height + 1)
        )
        extended = jnp.where(outside, jnp.zeros_like(hidden_fields), hidden_fields)
        forecast = (
            rows_first.astype(jnp.float32)
            + convolve(extended, conv2_weight)
            + conv2_bias
        ).astype(jnp.bfloat16)
        ensemble_part = forecast.shape[2]
        channels = forecast.shape[3]
        quarters = lax.psum(1, GRP)
        patch_width = forecast.shape[1] // quarters
        blocks = forecast.reshape(height, quarters, patch_width, ensemble_part, channels)
        row_index = lax.all_gather(obs_index, GRP, axis=0, tiled=False)
        column = row_index % patch_width
        channel = row_index // patch_width
        column_hot = (
            column[..., None] == jnp.arange(patch_width, dtype=jnp.int32)
        ).astype(jnp.bfloat16)
        by_column = jnp.einsum(
            "iqlmc,qiol->qicmo",
            blocks,
            column_hot,
            preferred_element_type=jnp.float32,
        )
        channel_hot = (
            channel[:, :, None, :] == jnp.arange(channels, dtype=jnp.int32)[None, None, :, None]
        ).astype(jnp.float32)
        own_members = jnp.sum(by_column * channel_hot[:, :, :, None, :], axis=2)
        predicted = lax.all_to_all(own_members, GRP, split_axis=0, concat_axis=2, tiled=True)[0]
        me = lax.axis_index(GRP)
        pieces = [lax.dynamic_index_in_dim(blocks, me, axis=1, keepdims=False)]
        for step in range(1, quarters):
            outgoing = lax.dynamic_index_in_dim(blocks, (me + step) % quarters, axis=1, keepdims=False)
            pieces.append(
                lax.ppermute(outgoing, GRP, [(j, (j + step) % quarters) for j in range(quarters)])
            )
        patch_block_slice = jnp.stack(pieces, axis=0)
        ensemble = quarters * ensemble_part
        source_member = (
            ((me - jnp.arange(quarters, dtype=jnp.int32)) % quarters)[:, None] * ensemble_part
            + jnp.arange(ensemble_part, dtype=jnp.int32)[None, :]
        ).reshape(ensemble)
        predicted_mean = jnp.mean(predicted, axis=1)
        perturb = predicted - predicted_mean[:, None, :]
        innovation = obs_values - predicted_mean
        gram_local = jnp.einsum(
            "pmo,po,pno->pmn", perturb, obs_prec, perturb, precision=highest
        )
        pull_vec = jnp.einsum(
            "pmo,po->pm", perturb, obs_prec * innovation, precision=highest
        )
        count = gram_local.shape[0]
        upper_rows, upper_cols = np.triu_indices(ensemble)
        upper = upper_rows * ensemble + upper_cols
        triangle = upper.shape[0]
        place_of = np.zeros((ensemble, ensemble), np.int32)
        place_of[upper_rows, upper_cols] = np.arange(triangle)
        place_of[upper_cols, upper_rows] = np.arange(triangle)
        packed = jnp.concatenate(
            [gram_local.reshape(count, ensemble * ensemble)[:, upper], pull_vec], axis=1
        )
        devices = lax.psum(1, GRP + BAND)
        packed = lax.all_to_all(
            jnp.broadcast_to(packed[None], (devices,) + packed.shape),
            GRP + BAND, split_axis=0, concat_axis=0, tiled=True,
        )
        packed = packed.reshape(-1, triangle + ensemble)
        total_patches = packed.shape[0]
        patch_ids = jnp.arange(total_patches, dtype=jnp.int32)
        matches = (neighbours[:, :, None] == patch_ids[None, None, :]).astype(jnp.float32)
        spread_weights = jnp.sum(loc_weight[:, :, None] * matches, axis=1)
        summed = jnp.einsum("pj,jf->pf", spread_weights, packed, precision=highest)
        gram_sum = summed[:, place_of.reshape(-1)].reshape(count, ensemble, ensemble)
        pull_sum = summed[:, triangle:]
        identity = jnp.broadcast_to(
            jnp.eye(ensemble, dtype=jnp.float32), (height, ensemble, ensemble)
        )
        matrix = (ensemble - 1.0) * identity + gram_local + gram_sum
        pulled = pull_vec + pull_sum
        norm_scale = jnp.sqrt(jnp.sum(matrix * matrix, axis=(1, 2)))
        sqrt_iter = matrix / norm_scale[:, None, None]
        inverse_root = identity
        for sweep in range(NS_ITERS):
            half_step = 1.5 * identity - 0.5 * jnp.einsum(
                "pab,pbc->pac", inverse_root, sqrt_iter, precision=highest
            )
            sqrt_iter = jnp.einsum("pab,pbc->pac", sqrt_iter, half_step, precision=highest)
            inverse_root = jnp.einsum("pab,pbc->pac", half_step, inverse_root, precision=highest)
        once_applied = jnp.einsum("pab,pb->pa", inverse_root, pulled, precision=highest)
        mean_weight = (
            jnp.einsum("pab,pb->pa", inverse_root, once_applied, precision=highest)
            / norm_scale[:, None]
        )
        transform = (jnp.sqrt(ensemble - 1.0) / jnp.sqrt(norm_scale))[
            :, None, None
        ] * inverse_root + mean_weight[:, :, None]
        weights = transform + (1.0 - jnp.sum(transform, axis=1, keepdims=True)) / ensemble
        weights = jnp.take(weights, source_member, axis=1).reshape(
            height, quarters, ensemble_part, ensemble
        )
        patch_of = jnp.arange(height, dtype=jnp.int32)
        spread_out = jnp.where(
            (patch_of[:, None] == patch_of[None, :])[None, :, :, None, None, None],
            patch_block_slice.astype(jnp.float32)[:, None],
            0.0,
        )
        analysed = jnp.einsum(
            "ajnm,jailnc->mcil", weights, spread_out, precision=highest
        )
        return analysed

    return on_device


def solution(mesh):
    grp_size, band_size = mesh.devices.shape
    fine = Mesh(
        mesh.devices.reshape(grp_size // 2, 2, 2, band_size // 32 * 4, 4),
        GRP + BAND,
    )
    placed = (
        P(BAND, None, GRP, None),
        P(),
        P(),
        P(),
        P(),
        P(GRP + BAND, None),
        P(GRP + BAND, None),
        P(GRP + BAND, None),
        P(GRP + BAND, None),
        P(GRP + BAND, None),
    )
    mapped = jax.shard_map(
        make_on_device(band_size),
        mesh=fine,
        in_specs=placed,
        out_specs=P(None, None, BAND, GRP),
        check_vma=False,
    )

    def run(prior_samples, *rest):
        rows_first = with_layout_constraint(
            jnp.transpose(prior_samples, (2, 3, 0, 1)), Layout((0, 1, 2, 3))
        )
        return mapped(rows_first, *rest)

    return run
```

```python
import jax
import jax.numpy as jnp
import numpy as np
from jax import lax
from jax.experimental.layout import Layout, with_layout_constraint
from jax.sharding import Mesh
from jax.sharding import PartitionSpec as P

NS_ITERS = 6

GRP = ("y_lo", "core")
BAND = ("y_hi", "x", "z")


def shift_pairs(count, step):
    return [(i, i + step) for i in range(count) if 0 <= i + step < count]


def padded_2(cells, band_size):
    return jnp.concatenate(
        [
            lax.ppermute(cells, BAND, shift_pairs(band_size, 1)),
            cells,
            lax.ppermute(cells, BAND, shift_pairs(band_size, -1)),
        ],
        axis=0,
    )


def convolve(padded, kernel):
    wrapped = jnp.concatenate([padded[:, -1:], padded, padded[:, :1]], axis=1)
    return lax.conv_general_dilated(
        wrapped,
        kernel,
        window_strides=(1, 1),
        padding="VALID",
        dimension_numbers=("HWNC", "HWOI", "HWNC"),
        preferred_element_type=jnp.float32,
    )


def make_on_device(band_size):
    def on_device(
        prior_samples,
        conv1_weight,
        conv1_bias,
        conv2_weight,
        conv2_bias,
        obs_index,
        obs_values,
        obs_prec,
        neighbours,
        loc_weight,
    ):
        highest = lax.Precision.HIGHEST
        rows_first = prior_samples
        height = rows_first.shape[0]
        padded = padded_2(rows_first, band_size)
        channels = rows_first.shape[3]
        hidden_fields = jax.nn.silu(
            convolve(padded, conv1_weight) + conv1_bias
        ).astype(jnp.bfloat16)
        place = lax.axis_index(BAND)
        row_ids = jnp.arange(height + 2, dtype=jnp.int32)[:, None, None, None]
        outside = ((place == 0) & (row_ids == 0)) | (
            (place == band_size - 1) & (row_ids == height + 1)
        )
        extended = jnp.where(outside, jnp.zeros_like(hidden_fields), hidden_fields)
        forecast = (
            rows_first.astype(jnp.float32)
            + convolve(
                extended,
                jnp.pad(conv2_weight, ((0, 0), (0, 0), (0, 128 - channels), (0, 0))),
            )[..., :channels]
            + conv2_bias
        ).astype(jnp.bfloat16)
        ensemble_part = forecast.shape[2]
        channels = forecast.shape[3]
        quarters = lax.psum(1, GRP)
        patch_width = forecast.shape[1] // quarters
        blocks = forecast.reshape(height, quarters, patch_width, ensemble_part, channels)
        row_index = lax.all_gather(obs_index, GRP, axis=0, tiled=False)
        column = row_index % patch_width
        channel = row_index // patch_width
        column_hot = (
            column[..., None] == jnp.arange(patch_width, dtype=jnp.int32)
        ).astype(jnp.bfloat16)
        by_column = jnp.einsum(
            "iqlmc,qiol->qicmo",
            blocks,
            column_hot,
            preferred_element_type=jnp.float32,
        )
        channel_hot = (
            channel[:, :, None, :] == jnp.arange(channels, dtype=jnp.int32)[None, None, :, None]
        ).astype(jnp.float32)
        own_members = jnp.sum(by_column * channel_hot[:, :, :, None, :], axis=2)
        predicted = lax.all_to_all(own_members, GRP, split_axis=0, concat_axis=2, tiled=True)[0]
        me = lax.axis_index(GRP)
        pieces = [lax.dynamic_index_in_dim(blocks, me, axis=1, keepdims=False)]
        for step in range(1, quarters):
            outgoing = lax.dynamic_index_in_dim(blocks, (me + step) % quarters, axis=1, keepdims=False)
            pieces.append(
                lax.ppermute(outgoing, GRP, [(j, (j + step) % quarters) for j in range(quarters)])
            )
        patch_block_slice = jnp.stack(pieces, axis=0)
        ensemble = quarters * ensemble_part
        source_member = (
            ((me - jnp.arange(quarters, dtype=jnp.int32)) % quarters)[:, None] * ensemble_part
            + jnp.arange(ensemble_part, dtype=jnp.int32)[None, :]
        ).reshape(ensemble)
        predicted_mean = jnp.mean(predicted, axis=1)
        perturb = predicted - predicted_mean[:, None, :]
        innovation = obs_values - predicted_mean
        gram_local = jnp.einsum(
            "pmo,po,pno->pmn", perturb, obs_prec, perturb, precision=highest
        )
        pull_vec = jnp.einsum(
            "pmo,po->pm", perturb, obs_prec * innovation, precision=highest
        )
        count = gram_local.shape[0]
        upper_rows, upper_cols = np.triu_indices(ensemble)
        upper = upper_rows * ensemble + upper_cols
        triangle = upper.shape[0]
        place_of = np.zeros((ensemble, ensemble), np.int32)
        place_of[upper_rows, upper_cols] = np.arange(triangle)
        place_of[upper_cols, upper_rows] = np.arange(triangle)
        packed = jnp.concatenate(
            [gram_local.reshape(count, ensemble * ensemble)[:, upper], pull_vec], axis=1
        )
        devices = lax.psum(1, GRP + BAND)
        packed = lax.all_to_all(
            jnp.broadcast_to(packed[None], (devices,) + packed.shape),
            GRP + BAND, split_axis=0, concat_axis=0, tiled=True,
        )
        packed = packed.reshape(-1, triangle + ensemble)
        total_patches = packed.shape[0]
        patch_ids = jnp.arange(total_patches, dtype=jnp.int32)
        matches = (neighbours[:, :, None] == patch_ids[None, None, :]).astype(jnp.float32)
        spread_weights = jnp.sum(loc_weight[:, :, None] * matches, axis=1)
        summed = jnp.einsum("pj,jf->pf", spread_weights, packed, precision=highest)
        gram_sum = summed[:, place_of.reshape(-1)].reshape(count, ensemble, ensemble)
        pull_sum = summed[:, triangle:]
        identity = jnp.broadcast_to(
            jnp.eye(ensemble, dtype=jnp.float32), (height, ensemble, ensemble)
        )
        matrix = (ensemble - 1.0) * identity + gram_local + gram_sum
        pulled = pull_vec + pull_sum
        norm_scale = jnp.sqrt(jnp.sum(matrix * matrix, axis=(1, 2)))
        sqrt_iter = matrix / norm_scale[:, None, None]
        inverse_root = identity
        for sweep in range(NS_ITERS):
            half_step = 1.5 * identity - 0.5 * jnp.einsum(
                "pab,pbc->pac", inverse_root, sqrt_iter, precision=highest
            )
            sqrt_iter = jnp.einsum("pab,pbc->pac", sqrt_iter, half_step, precision=highest)
            inverse_root = jnp.einsum("pab,pbc->pac", half_step, inverse_root, precision=highest)
        once_applied = jnp.einsum("pab,pb->pa", inverse_root, pulled, precision=highest)
        mean_weight = (
            jnp.einsum("pab,pb->pa", inverse_root, once_applied, precision=highest)
            / norm_scale[:, None]
        )
        transform = (jnp.sqrt(ensemble - 1.0) / jnp.sqrt(norm_scale))[
            :, None, None
        ] * inverse_root + mean_weight[:, :, None]
        weights = transform + (1.0 - jnp.sum(transform, axis=1, keepdims=True)) / ensemble
        weights = jnp.take(weights, source_member, axis=1).reshape(
            height, quarters, ensemble_part, ensemble
        )
        patch_of = jnp.arange(height, dtype=jnp.int32)
        spread_out = jnp.where(
            (patch_of[:, None] == patch_of[None, :])[None, :, :, None, None, None],
            patch_block_slice.astype(jnp.float32)[:, None],
            0.0,
        )
        analysed = jnp.einsum(
            "ajnm,jailnc->mcil", weights, spread_out, precision=highest
        )
        return analysed

    return on_device


def solution(mesh):
    grp_size, band_size = mesh.devices.shape
    fine = Mesh(
        mesh.devices.reshape(grp_size // 2, 2, 2, band_size // 32 * 4, 4),
        GRP + BAND,
    )
    placed = (
        P(BAND, None, GRP, None),
        P(),
        P(),
        P(),
        P(),
        P(GRP + BAND, None),
        P(GRP + BAND, None),
        P(GRP + BAND, None),
        P(GRP + BAND, None),
        P(GRP + BAND, None),
    )
    mapped = jax.shard_map(
        make_on_device(band_size),
        mesh=fine,
        in_specs=placed,
        out_specs=P(None, None, BAND, GRP),
        check_vma=False,
    )

    def run(prior_samples, *rest):
        rows_first = with_layout_constraint(
            jnp.transpose(prior_samples, (2, 3, 0, 1)), Layout((0, 1, 2, 3))
        )
        return mapped(rows_first, *rest)

    return run
```

```python
import jax
import jax.numpy as jnp
import numpy as np
from jax import lax
from jax.experimental.layout import Layout, with_layout_constraint
from jax.sharding import Mesh
from jax.sharding import PartitionSpec as P

NS_ITERS = 6

GRP = ("y_lo", "core")
BAND = ("y_hi", "x", "z")


def shift_pairs(count, step):
    return [(i, i + step) for i in range(count) if 0 <= i + step < count]


def padded_2(cells, band_size):
    return jnp.concatenate(
        [
            lax.ppermute(cells, BAND, shift_pairs(band_size, 1)),
            cells,
            lax.ppermute(cells, BAND, shift_pairs(band_size, -1)),
        ],
        axis=0,
    )


def convolve(padded, kernel):
    wrapped = jnp.concatenate([padded[:, -1:], padded, padded[:, :1]], axis=1)
    return lax.conv_general_dilated(
        wrapped,
        kernel,
        window_strides=(1, 1),
        padding="VALID",
        dimension_numbers=("HWNC", "HWOI", "HWNC"),
        preferred_element_type=jnp.float32,
    )


def make_on_device(band_size):
    def on_device(
        prior_samples,
        conv1_weight,
        conv1_bias,
        conv2_weight,
        conv2_bias,
        obs_index,
        obs_values,
        obs_prec,
        neighbours,
        loc_weight,
    ):
        highest = lax.Precision.HIGHEST
        rows_first = prior_samples
        height = rows_first.shape[0]
        padded = padded_2(rows_first, band_size)
        channels = rows_first.shape[3]
        hidden_fields = jax.nn.silu(
            convolve(padded, conv1_weight) + conv1_bias
        ).astype(jnp.bfloat16)
        place = lax.axis_index(BAND)
        row_ids = jnp.arange(height + 2, dtype=jnp.int32)[:, None, None, None]
        outside = ((place == 0) & (row_ids == 0)) | (
            (place == band_size - 1) & (row_ids == height + 1)
        )
        extended = jnp.where(outside, jnp.zeros_like(hidden_fields), hidden_fields)
        forecast = (
            rows_first.astype(jnp.float32)
            + convolve(
                extended,
                jnp.pad(conv2_weight, ((0, 0), (0, 0), (0, 128 - channels), (0, 0))),
            )[..., :channels]
            + conv2_bias
        ).astype(jnp.bfloat16)
        ensemble_part = forecast.shape[2]
        channels = forecast.shape[3]
        quarters = lax.psum(1, GRP)
        patch_width = forecast.shape[1] // quarters
        blocks = forecast.reshape(height, quarters, patch_width, ensemble_part, channels)
        row_index = lax.all_gather(obs_index, GRP, axis=0, tiled=False)
        column = row_index % patch_width
        channel = row_index // patch_width
        column_hot = (
            column[..., None] == jnp.arange(patch_width, dtype=jnp.int32)
        ).astype(jnp.bfloat16)
        by_column = jnp.einsum(
            "iqlmc,qiol->qicmo",
            blocks,
            column_hot,
            preferred_element_type=jnp.float32,
        )
        channel_hot = (
            channel[:, :, None, :] == jnp.arange(channels, dtype=jnp.int32)[None, None, :, None]
        ).astype(jnp.float32)
        own_members = jnp.sum(by_column * channel_hot[:, :, :, None, :], axis=2)
        predicted = lax.all_to_all(own_members, GRP, split_axis=0, concat_axis=2, tiled=True)[0]
        me = lax.axis_index(GRP)
        pieces = [lax.dynamic_index_in_dim(blocks, me, axis=1, keepdims=False)]
        for step in range(1, quarters):
            outgoing = lax.dynamic_index_in_dim(blocks, (me + step) % quarters, axis=1, keepdims=False)
            pieces.append(
                lax.ppermute(outgoing, GRP, [(j, (j + step) % quarters) for j in range(quarters)])
            )
        patch_block_slice = jnp.stack(pieces, axis=0)
        ensemble = quarters * ensemble_part
        source_member = (
            ((me - jnp.arange(quarters, dtype=jnp.int32)) % quarters)[:, None] * ensemble_part
            + jnp.arange(ensemble_part, dtype=jnp.int32)[None, :]
        ).reshape(ensemble)
        predicted_mean = jnp.mean(predicted, axis=1)
        perturb = predicted - predicted_mean[:, None, :]
        innovation = obs_values - predicted_mean
        gram_local = jnp.einsum(
            "pmo,po,pno->pmn", perturb, obs_prec, perturb, precision=highest
        )
        pull_vec = jnp.einsum(
            "pmo,po->pm", perturb, obs_prec * innovation, precision=highest
        )
        count = gram_local.shape[0]
        upper_rows, upper_cols = np.triu_indices(ensemble)
        upper = upper_rows * ensemble + upper_cols
        triangle = upper.shape[0]
        place_of = np.zeros((ensemble, ensemble), np.int32)
        place_of[upper_rows, upper_cols] = np.arange(triangle)
        place_of[upper_cols, upper_rows] = np.arange(triangle)
        packed = jnp.concatenate(
            [gram_local.reshape(count, ensemble * ensemble)[:, upper], pull_vec], axis=1
        )
        devices = lax.psum(1, GRP + BAND)
        packed = lax.all_to_all(
            jnp.broadcast_to(packed[None], (devices,) + packed.shape),
            GRP + BAND, split_axis=0, concat_axis=0, tiled=True,
        )
        packed = packed.reshape(-1, triangle + ensemble)
        total_patches = packed.shape[0]
        patch_ids = jnp.arange(total_patches, dtype=jnp.int32)
        matches = (neighbours[:, :, None] == patch_ids[None, None, :]).astype(jnp.float32)
        spread_weights = jnp.sum(loc_weight[:, :, None] * matches, axis=1)
        summed = jnp.einsum("pj,jf->pf", spread_weights, packed, precision=highest)
        gram_sum = summed[:, place_of.reshape(-1)].reshape(count, ensemble, ensemble)
        pull_sum = summed[:, triangle:]
        identity = jnp.broadcast_to(
            jnp.eye(ensemble, dtype=jnp.float32), (height, ensemble, ensemble)
        )
        matrix = (ensemble - 1.0) * identity + gram_local + gram_sum
        pulled = pull_vec + pull_sum
        norm_scale = jnp.sqrt(jnp.sum(matrix * matrix, axis=(1, 2)))
        sqrt_iter = matrix / norm_scale[:, None, None]
        inverse_root = identity
        for sweep in range(NS_ITERS):
            half_step = 1.5 * identity - 0.5 * jnp.einsum(
                "pab,pbc->pac", inverse_root, sqrt_iter, precision=highest
            )
            both = jnp.einsum(
                "pab,pbc->pac",
                half_step,
                jnp.concatenate([sqrt_iter, inverse_root], axis=2),
                precision=highest,
            )
            sqrt_iter = both[:, :, :ensemble]
            inverse_root = both[:, :, ensemble:]
        once_applied = jnp.einsum("pab,pb->pa", inverse_root, pulled, precision=highest)
        mean_weight = (
            jnp.einsum("pab,pb->pa", inverse_root, once_applied, precision=highest)
            / norm_scale[:, None]
        )
        transform = (jnp.sqrt(ensemble - 1.0) / jnp.sqrt(norm_scale))[
            :, None, None
        ] * inverse_root + mean_weight[:, :, None]
        weights = transform + (1.0 - jnp.sum(transform, axis=1, keepdims=True)) / ensemble
        weights = jnp.take(weights, source_member, axis=1).reshape(
            height, quarters, ensemble_part, ensemble
        )
        patch_of = jnp.arange(height, dtype=jnp.int32)
        spread_out = jnp.where(
            (patch_of[:, None] == patch_of[None, :])[None, :, :, None, None, None],
            patch_block_slice.astype(jnp.float32)[:, None],
            0.0,
        )
        analysed = jnp.einsum(
            "ajnm,jailnc->mcil", weights, spread_out, precision=highest
        )
        return analysed

    return on_device


def solution(mesh):
    grp_size, band_size = mesh.devices.shape
    fine = Mesh(
        mesh.devices.reshape(grp_size // 2, 2, 2, band_size // 32 * 4, 4),
        GRP + BAND,
    )
    placed = (
        P(BAND, None, GRP, None),
        P(),
        P(),
        P(),
        P(),
        P(GRP + BAND, None),
        P(GRP + BAND, None),
        P(GRP + BAND, None),
        P(GRP + BAND, None),
        P(GRP + BAND, None),
    )
    mapped = jax.shard_map(
        make_on_device(band_size),
        mesh=fine,
        in_specs=placed,
        out_specs=P(None, None, BAND, GRP),
        check_vma=False,
    )

    def run(prior_samples, *rest):
        rows_first = with_layout_constraint(
            jnp.transpose(prior_samples, (2, 3, 0, 1)), Layout((0, 1, 2, 3))
        )
        return mapped(rows_first, *rest)

    return run
```

```python
import jax
import jax.numpy as jnp
import numpy as np
from jax import lax
from jax.experimental.layout import Layout, with_layout_constraint
from jax.sharding import Mesh
from jax.sharding import PartitionSpec as P

NS_ITERS = 6

GRP = ("y_lo", "core")
BAND = ("y_hi", "x", "z")


def shift_pairs(count, step):
    return [(i, i + step) for i in range(count) if 0 <= i + step < count]


def padded_2(cells, band_size):
    return jnp.concatenate(
        [
            lax.ppermute(cells, BAND, shift_pairs(band_size, 1)),
            cells,
            lax.ppermute(cells, BAND, shift_pairs(band_size, -1)),
        ],
        axis=0,
    )


def convolve(padded, kernel):
    wrapped = jnp.concatenate([padded[:, -1:], padded, padded[:, :1]], axis=1)
    return lax.conv_general_dilated(
        wrapped,
        kernel,
        window_strides=(1, 1),
        padding="VALID",
        dimension_numbers=("HWNC", "HWOI", "HWNC"),
        preferred_element_type=jnp.float32,
    )


def make_on_device(band_size):
    def on_device(
        prior_samples,
        conv1_weight,
        conv1_bias,
        conv2_weight,
        conv2_bias,
        obs_index,
        obs_values,
        obs_prec,
        neighbours,
        loc_weight,
    ):
        highest = lax.Precision.HIGHEST
        rows_first = prior_samples
        height = rows_first.shape[0]
        padded = padded_2(rows_first, band_size)
        hidden_fields = jax.nn.silu(
            convolve(padded, conv1_weight) + conv1_bias
        ).astype(jnp.bfloat16)
        place = lax.axis_index(BAND)
        row_ids = jnp.arange(height + 2, dtype=jnp.int32)[:, None, None, None]
        outside = ((place == 0) & (row_ids == 0)) | (
            (place == band_size - 1) & (row_ids == height + 1)
        )
        extended = jnp.where(outside, jnp.zeros_like(hidden_fields), hidden_fields)
        forecast = (
            rows_first.astype(jnp.float32)
            + convolve(extended, conv2_weight)
            + conv2_bias
        ).astype(jnp.bfloat16)
        ensemble_part = forecast.shape[2]
        channels = forecast.shape[3]
        quarters = lax.psum(1, GRP)
        patch_width = forecast.shape[1] // quarters
        blocks = forecast.reshape(height, quarters, patch_width, ensemble_part, channels)
        row_index = lax.all_gather(obs_index, GRP, axis=0, tiled=False)
        column = row_index % patch_width
        channel = row_index // patch_width
        column_hot = (
            column[..., None] == jnp.arange(patch_width, dtype=jnp.int32)
        ).astype(jnp.bfloat16)
        by_column = jnp.einsum(
            "iqlmc,qiol->qicmo",
            blocks,
            column_hot,
            preferred_element_type=jnp.float32,
        )
        channel_hot = (
            channel[:, :, None, :] == jnp.arange(channels, dtype=jnp.int32)[None, None, :, None]
        ).astype(jnp.float32)
        own_members = jnp.sum(by_column * channel_hot[:, :, :, None, :], axis=2)
        predicted = lax.all_to_all(own_members, GRP, split_axis=0, concat_axis=2, tiled=True)[0]
        me = lax.axis_index(GRP)
        pieces = [lax.dynamic_index_in_dim(blocks, me, axis=1, keepdims=False)]
        for step in range(1, quarters):
            outgoing = lax.dynamic_index_in_dim(blocks, (me + step) % quarters, axis=1, keepdims=False)
            pieces.append(
                lax.ppermute(outgoing, GRP, [(j, (j + step) % quarters) for j in range(quarters)])
            )
        patch_block_slice = jnp.stack(pieces, axis=0)
        ensemble = quarters * ensemble_part
        source_member = (
            ((me - jnp.arange(quarters, dtype=jnp.int32)) % quarters)[:, None] * ensemble_part
            + jnp.arange(ensemble_part, dtype=jnp.int32)[None, :]
        ).reshape(ensemble)
        predicted_mean = jnp.mean(predicted, axis=1)
        perturb = predicted - predicted_mean[:, None, :]
        innovation = obs_values - predicted_mean
        gram_local = jnp.einsum(
            "pmo,po,pno->pmn", perturb, obs_prec, perturb, precision=highest
        )
        pull_vec = jnp.einsum(
            "pmo,po->pm", perturb, obs_prec * innovation, precision=highest
        )
        count = gram_local.shape[0]
        upper_rows, upper_cols = np.triu_indices(ensemble)
        upper = upper_rows * ensemble + upper_cols
        triangle = upper.shape[0]
        place_of = np.zeros((ensemble, ensemble), np.int32)
        place_of[upper_rows, upper_cols] = np.arange(triangle)
        place_of[upper_cols, upper_rows] = np.arange(triangle)
        packed = jnp.concatenate(
            [gram_local.reshape(count, ensemble * ensemble)[:, upper], pull_vec], axis=1
        )
        devices = lax.psum(1, GRP + BAND)
        packed = lax.all_to_all(
            jnp.broadcast_to(packed[None], (devices,) + packed.shape),
            GRP + BAND, split_axis=0, concat_axis=0, tiled=True,
        )
        packed = packed.reshape(-1, triangle + ensemble)
        total_patches = packed.shape[0]
        patch_ids = jnp.arange(total_patches, dtype=jnp.int32)
        matches = (neighbours[:, :, None] == patch_ids[None, None, :]).astype(jnp.float32)
        spread_weights = jnp.sum(loc_weight[:, :, None] * matches, axis=1)
        summed = jnp.einsum("pj,jf->pf", spread_weights, packed, precision=highest)
        gram_sum = summed[:, place_of.reshape(-1)].reshape(count, ensemble, ensemble)
        pull_sum = summed[:, triangle:]
        identity = jnp.broadcast_to(
            jnp.eye(ensemble, dtype=jnp.float32), (height, ensemble, ensemble)
        )
        matrix = (ensemble - 1.0) * identity + gram_local + gram_sum
        pulled = pull_vec + pull_sum
        norm_scale = jnp.sqrt(jnp.sum(matrix * matrix, axis=(1, 2)))
        sqrt_iter = matrix / norm_scale[:, None, None]
        inverse_root = identity
        for sweep in range(NS_ITERS):
            half_step = 1.5 * identity - 0.5 * jnp.einsum(
                "pab,pbc->pac", inverse_root, sqrt_iter, precision=highest
            )
            sqrt_iter = jnp.einsum("pab,pbc->pac", sqrt_iter, half_step, precision=highest)
            inverse_root = jnp.einsum("pab,pbc->pac", half_step, inverse_root, precision=highest)
        once_applied = jnp.einsum("pab,pb->pa", inverse_root, pulled, precision=highest)
        mean_weight = (
            jnp.einsum("pab,pb->pa", inverse_root, once_applied, precision=highest)
            / norm_scale[:, None]
        )
        transform = (jnp.sqrt(ensemble - 1.0) / jnp.sqrt(norm_scale))[
            :, None, None
        ] * inverse_root + mean_weight[:, :, None]
        weights = transform + (1.0 - jnp.sum(transform, axis=1, keepdims=True)) / ensemble
        weights = jnp.take(weights, source_member, axis=1).reshape(
            height, quarters, ensemble_part, ensemble
        )
        patch_of = jnp.arange(height, dtype=jnp.int32)
        spread_out = jnp.where(
            (patch_of[:, None] == patch_of[None, :])[None, :, :, None, None, None],
            patch_block_slice.astype(jnp.float32)[:, None],
            0.0,
        )
        analysed = jnp.einsum(
            "ajnm,jailnc->mcil", weights, spread_out, precision=lax.Precision.HIGH
        )
        return analysed

    return on_device


def solution(mesh):
    grp_size, band_size = mesh.devices.shape
    fine = Mesh(
        mesh.devices.reshape(grp_size // 2, 2, 2, band_size // 32 * 4, 4),
        GRP + BAND,
    )
    placed = (
        P(BAND, None, GRP, None),
        P(),
        P(),
        P(),
        P(),
        P(GRP + BAND, None),
        P(GRP + BAND, None),
        P(GRP + BAND, None),
        P(GRP + BAND, None),
        P(GRP + BAND, None),
    )
    mapped = jax.shard_map(
        make_on_device(band_size),
        mesh=fine,
        in_specs=placed,
        out_specs=P(None, None, BAND, GRP),
        check_vma=False,
    )

    def run(prior_samples, *rest):
        rows_first = with_layout_constraint(
            jnp.transpose(prior_samples, (2, 3, 0, 1)), Layout((0, 1, 2, 3))
        )
        return mapped(rows_first, *rest)

    return run
```

```python
import jax
import jax.numpy as jnp
import numpy as np
from jax import lax
from jax.experimental.layout import Layout, with_layout_constraint
from jax.sharding import Mesh
from jax.sharding import PartitionSpec as P

NS_ITERS = 6

GRP = ("y_lo", "core")
BAND = ("y_hi", "x", "z")


def shift_pairs(count, step):
    return [(i, i + step) for i in range(count) if 0 <= i + step < count]


def padded_2(cells, band_size):
    return jnp.concatenate(
        [
            lax.ppermute(cells, BAND, shift_pairs(band_size, 1)),
            cells,
            lax.ppermute(cells, BAND, shift_pairs(band_size, -1)),
        ],
        axis=0,
    )


def convolve(padded, kernel):
    wrapped = jnp.concatenate([padded[:, -1:], padded, padded[:, :1]], axis=1)
    return lax.conv_general_dilated(
        wrapped,
        kernel,
        window_strides=(1, 1),
        padding="VALID",
        dimension_numbers=("HWNC", "HWOI", "HWNC"),
        preferred_element_type=jnp.float32,
    )


def make_on_device(band_size):
    def on_device(
        prior_samples,
        conv1_weight,
        conv1_bias,
        conv2_weight,
        conv2_bias,
        obs_index,
        obs_values,
        obs_prec,
        neighbours,
        loc_weight,
    ):
        highest = lax.Precision.HIGH
        rows_first = prior_samples
        height = rows_first.shape[0]
        padded = padded_2(rows_first, band_size)
        hidden_fields = jax.nn.silu(
            convolve(padded, conv1_weight) + conv1_bias
        ).astype(jnp.bfloat16)
        place = lax.axis_index(BAND)
        row_ids = jnp.arange(height + 2, dtype=jnp.int32)[:, None, None, None]
        outside = ((place == 0) & (row_ids == 0)) | (
            (place == band_size - 1) & (row_ids == height + 1)
        )
        extended = jnp.where(outside, jnp.zeros_like(hidden_fields), hidden_fields)
        forecast = (
            rows_first.astype(jnp.float32)
            + convolve(extended, conv2_weight)
            + conv2_bias
        ).astype(jnp.bfloat16)
        ensemble_part = forecast.shape[2]
        channels = forecast.shape[3]
        quarters = lax.psum(1, GRP)
        patch_width = forecast.shape[1] // quarters
        blocks = forecast.reshape(height, quarters, patch_width, ensemble_part, channels)
        row_index = lax.all_gather(obs_index, GRP, axis=0, tiled=False)
        column = row_index % patch_width
        channel = row_index // patch_width
        column_hot = (
            column[..., None] == jnp.arange(patch_width, dtype=jnp.int32)
        ).astype(jnp.bfloat16)
        by_column = jnp.einsum(
            "iqlmc,qiol->qicmo",
            blocks,
            column_hot,
            preferred_element_type=jnp.float32,
        )
        channel_hot = (
            channel[:, :, None, :] == jnp.arange(channels, dtype=jnp.int32)[None, None, :, None]
        ).astype(jnp.float32)
        own_members = jnp.sum(by_column * channel_hot[:, :, :, None, :], axis=2)
        predicted = lax.all_to_all(own_members, GRP, split_axis=0, concat_axis=2, tiled=True)[0]
        me = lax.axis_index(GRP)
        pieces = [lax.dynamic_index_in_dim(blocks, me, axis=1, keepdims=False)]
        for step in range(1, quarters):
            outgoing = lax.dynamic_index_in_dim(blocks, (me + step) % quarters, axis=1, keepdims=False)
            pieces.append(
                lax.ppermute(outgoing, GRP, [(j, (j + step) % quarters) for j in range(quarters)])
            )
        patch_block_slice = jnp.stack(pieces, axis=0)
        ensemble = quarters * ensemble_part
        source_member = (
            ((me - jnp.arange(quarters, dtype=jnp.int32)) % quarters)[:, None] * ensemble_part
            + jnp.arange(ensemble_part, dtype=jnp.int32)[None, :]
        ).reshape(ensemble)
        predicted_mean = jnp.mean(predicted, axis=1)
        perturb = predicted - predicted_mean[:, None, :]
        innovation = obs_values - predicted_mean
        gram_local = jnp.einsum(
            "pmo,po,pno->pmn", perturb, obs_prec, perturb, precision=highest
        )
        pull_vec = jnp.einsum(
            "pmo,po->pm", perturb, obs_prec * innovation, precision=highest
        )
        count = gram_local.shape[0]
        upper_rows, upper_cols = np.triu_indices(ensemble)
        upper = upper_rows * ensemble + upper_cols
        triangle = upper.shape[0]
        place_of = np.zeros((ensemble, ensemble), np.int32)
        place_of[upper_rows, upper_cols] = np.arange(triangle)
        place_of[upper_cols, upper_rows] = np.arange(triangle)
        packed = jnp.concatenate(
            [gram_local.reshape(count, ensemble * ensemble)[:, upper], pull_vec], axis=1
        )
        devices = lax.psum(1, GRP + BAND)
        packed = lax.all_to_all(
            jnp.broadcast_to(packed[None], (devices,) + packed.shape),
            GRP + BAND, split_axis=0, concat_axis=0, tiled=True,
        )
        packed = packed.reshape(-1, triangle + ensemble)
        total_patches = packed.shape[0]
        patch_ids = jnp.arange(total_patches, dtype=jnp.int32)
        matches = (neighbours[:, :, None] == patch_ids[None, None, :]).astype(jnp.float32)
        spread_weights = jnp.sum(loc_weight[:, :, None] * matches, axis=1)
        summed = jnp.einsum("pj,jf->pf", spread_weights, packed, precision=highest)
        gram_sum = summed[:, place_of.reshape(-1)].reshape(count, ensemble, ensemble)
        pull_sum = summed[:, triangle:]
        identity = jnp.broadcast_to(
            jnp.eye(ensemble, dtype=jnp.float32), (height, ensemble, ensemble)
        )
        matrix = (ensemble - 1.0) * identity + gram_local + gram_sum
        pulled = pull_vec + pull_sum
        norm_scale = jnp.sqrt(jnp.sum(matrix * matrix, axis=(1, 2)))
        sqrt_iter = matrix / norm_scale[:, None, None]
        inverse_root = identity
        for sweep in range(NS_ITERS):
            half_step = 1.5 * identity - 0.5 * jnp.einsum(
                "pab,pbc->pac", inverse_root, sqrt_iter, precision=highest
            )
            sqrt_iter = jnp.einsum("pab,pbc->pac", sqrt_iter, half_step, precision=highest)
            inverse_root = jnp.einsum("pab,pbc->pac", half_step, inverse_root, precision=highest)
        once_applied = jnp.einsum("pab,pb->pa", inverse_root, pulled, precision=highest)
        mean_weight = (
            jnp.einsum("pab,pb->pa", inverse_root, once_applied, precision=highest)
            / norm_scale[:, None]
        )
        transform = (jnp.sqrt(ensemble - 1.0) / jnp.sqrt(norm_scale))[
            :, None, None
        ] * inverse_root + mean_weight[:, :, None]
        weights = transform + (1.0 - jnp.sum(transform, axis=1, keepdims=True)) / ensemble
        weights = jnp.take(weights, source_member, axis=1).reshape(
            height, quarters, ensemble_part, ensemble
        )
        patch_of = jnp.arange(height, dtype=jnp.int32)
        spread_out = jnp.where(
            (patch_of[:, None] == patch_of[None, :])[None, :, :, None, None, None],
            patch_block_slice.astype(jnp.float32)[:, None],
            0.0,
        )
        analysed = jnp.einsum(
            "ajnm,jailnc->mcil", weights, spread_out, precision=lax.Precision.HIGH
        )
        return analysed

    return on_device


def solution(mesh):
    grp_size, band_size = mesh.devices.shape
    fine = Mesh(
        mesh.devices.reshape(grp_size // 2, 2, 2, band_size // 32 * 4, 4),
        GRP + BAND,
    )
    placed = (
        P(BAND, None, GRP, None),
        P(),
        P(),
        P(),
        P(),
        P(GRP + BAND, None),
        P(GRP + BAND, None),
        P(GRP + BAND, None),
        P(GRP + BAND, None),
        P(GRP + BAND, None),
    )
    mapped = jax.shard_map(
        make_on_device(band_size),
        mesh=fine,
        in_specs=placed,
        out_specs=P(None, None, BAND, GRP),
        check_vma=False,
    )

    def run(prior_samples, *rest):
        rows_first = with_layout_constraint(
            jnp.transpose(prior_samples, (2, 3, 0, 1)), Layout((0, 1, 2, 3))
        )
        return mapped(rows_first, *rest)

    return run
```
